256 devices in a mesh: row: 16 (over y, x), col: 16 (over z, core).
Axes of the slice: x: 4, y: 4, z: 8, core: 2. Of those that a mesh axis runs over, the one named last changes fastest.
Arguments:
- features: float32 [65536, 512], P(('col', 'row')), may hold values from -6 to 6
- weight: float32 [512, 512], replicated, may hold values from -0.25 to 0.25
- tile_values: bfloat16 [16, 16, 32, 256, 256], P('row', 'col'), as said below
- tile_ids: int32 [16, 16, 32, 2], P('row', 'col'), may hold values from 0 to 15, as said below
- tile_counts: int32 [16, 16], P('row', 'col'), may hold values from 1 to 32, as said below
Outputs:
- activated: float32 [65536, 512], P(('row', 'col'))
The draws below stay inside these ranges and needn't reach their ends.
Inputs may be any that keep to these rules, and one draw needn't show every extreme that they name: `tile_counts`: slots at or beyond a panel's count are ignored; some panel holds 32 live slots. `tile_ids`: the first entry is below 16, the second below 16; a tile may repeat. `tile_values`: nonnegative.
All inputs are finite; a program needn't handle non-finite values.
Results may differ from the reference program's by a relative error of at most 0.0003.
Values may be sent and summed in bfloat16 or wider, within the bound.
No kernel may reach another device: no remote copies, remote signals or barrier semaphores. Data moves between devices by JAX's collectives and lax.ppermute only.
A program may use at most 128 MiB of HBM per device.

```python
import jax
import jax.numpy as jnp
from jax import lax

TILE_EDGE = 256
F = 512
DEVICE_TILES = 32
N = 65536
RPB = 16
COLUMNS_PER_PANEL = 16
N_ROW = 16
N_COL = 16


def draw_tile_counts(key, part):
    key_first, key_second, key_chosen = jax.random.split(key, 3)
    first_draw = jax.random.randint(key_first, (N_ROW * N_COL,), 1, DEVICE_TILES + 1)
    second_draw = jax.random.randint(key_second, (N_ROW * N_COL,), 1, DEVICE_TILES + 1)
    smaller = jnp.minimum(first_draw, second_draw)
    chosen = jax.random.randint(key_chosen, (), 0, N_ROW * N_COL)
    smaller = smaller.at[chosen].set(DEVICE_TILES)
    return smaller.reshape(N_ROW, N_COL).astype(jnp.int32)


def draw_tile_ids(key, part):
    key_rows, key_columns = jax.random.split(jax.random.fold_in(key, 11), 2)
    row_part = jax.random.randint(key_rows, (N_ROW, N_COL, DEVICE_TILES), 0, RPB)
    column_portion = jax.random.randint(key_columns, (N_ROW, N_COL, DEVICE_TILES), 0, COLUMNS_PER_PANEL)
    return jnp.stack([row_part, column_portion], axis=-1).astype(jnp.int32)


def draw_tile_values(key, part):
    key_base, key_rows, key_columns = jax.random.split(jax.random.fold_in(key, 23), 3)
    base = jax.random.uniform(key_base, (N_ROW, N_COL, DEVICE_TILES, TILE_EDGE, TILE_EDGE), jnp.float32)
    row_scale = jnp.exp(jax.random.uniform(key_rows, (N_ROW, N_COL, DEVICE_TILES, TILE_EDGE, 1), jnp.float32) * 2.302585) * 0.1
    col_scale = jnp.exp(jax.random.uniform(key_columns, (N_ROW, N_COL, DEVICE_TILES, 1, TILE_EDGE), jnp.float32) * 2.302585) * 0.1
    ramp = 1.0 + 2.0 * jnp.arange(N_COL, dtype=jnp.float32) / max(N_COL - 1, 1)
    values = base * row_scale * col_scale * ramp[None, :, None, None, None]
    return values.astype(jnp.bfloat16)


def steps_of(stream_key, shape, cuts, least, high):
    def one(position, shards_of):
        heights = jax.random.uniform(jax.random.fold_in(jax.random.fold_in(stream_key, 6), position), (shards_of,), jnp.float32, least / len(cuts), high / len(cuts))
        return jnp.repeat(jnp.exp(heights), shape[position] // shards_of).reshape((-1,) + (1,) * (len(shape) - position - 1))

    factor_of = one(*cuts[0])
    for cut in cuts[1:]:
        factor_of = factor_of * one(*cut)
    return factor_of


def scatter_about(stream_key, extent, width, reach, cuts=(), kind=jnp.bfloat16):
    gain = steps_of(stream_key, extent, cuts, -0.22, 0.18) if cuts else 1.0
    values = jax.random.normal(stream_key, extent, jnp.float32) * width * gain
    return jnp.minimum(jnp.maximum(values, -reach), reach).astype(kind)


def setup_inputs(seed: int = 0) -> dict:
    key_of = jax.random.split(jax.random.key(seed), 6)
    features = scatter_about(key_of[0], (N, F), 1.0, 6.0, ((0, 256),), jnp.float32)
    weight = scatter_about(key_of[1], (F, F), F ** -0.5, 0.25, (), jnp.float32)
    tile_values = draw_tile_values(jax.random.fold_in(key_of[5], 71), 0)
    tile_ids = draw_tile_ids(jax.random.fold_in(key_of[5], 71), 0)
    tile_counts = draw_tile_counts(jax.random.fold_in(key_of[5], 71), 0)
    return {"features": features, "weight": weight, "tile_values": tile_values, "tile_ids": tile_ids, "tile_counts": tile_counts}


def reference(features, weight, tile_values, tile_ids, tile_counts):
    flat_values = tile_values.reshape(N_ROW * N_COL * DEVICE_TILES, TILE_EDGE, TILE_EDGE)
    flattened_ids = tile_ids.reshape(N_ROW * N_COL * DEVICE_TILES, 2)
    panel_counts = tile_counts.reshape(N_ROW * N_COL)

    def visit_slot(flattened_index, running):
        device = flattened_index // DEVICE_TILES
        slot_index = flattened_index % DEVICE_TILES
        grid_row = device // N_COL
        column_in_grid = device % N_COL

        def apply_tile(state_pair):
            summed, degree = state_pair
            tile_block = flat_values[flattened_index].astype(jnp.float32)
            row_start = ((grid_row * RPB + flattened_ids[flattened_index, 0]) * TILE_EDGE).astype(jnp.int32)
            column_begin = ((column_in_grid * COLUMNS_PER_PANEL + flattened_ids[flattened_index, 1]) * TILE_EDGE).astype(jnp.int32)
            source_rows = lax.dynamic_slice_in_dim(features, column_begin, TILE_EDGE, 0)
            product = jnp.dot(tile_block, source_rows, precision=lax.Precision.HIGHEST)
            old_rows = lax.dynamic_slice_in_dim(summed, row_start, TILE_EDGE, 0)
            summed = lax.dynamic_update_slice_in_dim(summed, old_rows + product, row_start, 0)
            old_degree = lax.dynamic_slice_in_dim(degree, row_start, TILE_EDGE, 0)
            degree = lax.dynamic_update_slice_in_dim(degree, old_degree + lax.optimization_barrier(jnp.sum(tile_block, axis=1)), row_start, 0)
            return (summed, degree)

        def unchanged(state_pair):
            return state_pair
        return lax.cond(slot_index < panel_counts[device], apply_tile, unchanged, running)
    start_pair = (features.astype(jnp.float32), jnp.ones((N,), jnp.float32))
    summed, degree = lax.fori_loop(0, N_ROW * N_COL * DEVICE_TILES, visit_slot, start_pair)
    projected = jnp.dot(summed, weight, precision=lax.Precision.HIGHEST)
    return jnp.maximum(projected * lax.rsqrt(degree)[:, None], 0.0)
```

```python
import jax
import jax.numpy as jnp
from jax import lax
from jax.experimental import pallas as pl
from jax.experimental.pallas import tpu as pltpu
from jax.sharding import PartitionSpec as P

EXTRA = 8


def _split3(x):
    hi = x.astype(jnp.bfloat16)
    r1 = x - hi.astype(jnp.float32)
    mid = r1.astype(jnp.bfloat16)
    lo = (r1 - mid.astype(jnp.float32)).astype(jnp.bfloat16)
    return hi, mid, lo


def _tile_kernel(ids_ref, cnt_ref, flag_ref, tile_ref, x_ref, out_ref):
    s = pl.program_id(0)
    edge = tile_ref.shape[1]
    blocks = out_ref.shape[0]

    @pl.when(s == 0)
    def _init():
        own = x_ref[...].reshape(blocks, edge, x_ref.shape[1])
        keep = flag_ref[0] != 0
        out_ref[:, :edge, :] = jnp.where(keep, own, jnp.zeros_like(own))
        out_ref[:, edge:, :] = jnp.zeros((blocks, EXTRA, out_ref.shape[2]), jnp.float32)

    @pl.when(s < cnt_ref[0])
    def _add():
        i = ids_ref[2 * s]
        j = ids_ref[2 * s + 1]
        tile = tile_ref[0]
        start = pl.multiple_of(j * edge, edge)
        xb = x_ref[pl.ds(start, edge), :]
        hi, mid, lo = _split3(xb)
        prod = jnp.dot(tile, hi, preferred_element_type=jnp.float32)
        prod += jnp.dot(tile, mid, preferred_element_type=jnp.float32)
        prod += jnp.dot(tile, lo, preferred_element_type=jnp.float32)
        out_ref[i, :edge, :] += prod
        first = (lax.broadcasted_iota(jnp.int32, (EXTRA, edge), 0) == 0).astype(jnp.bfloat16)
        sums = lax.dot_general(
            first, tile, (((1,), (1,)), ((), ())), preferred_element_type=jnp.float32
        )
        out_ref[i, edge:, :edge] += sums


def _panel_products(ids, cnt, flag, tile_set, panel):
    slots, edge, _ = tile_set.shape
    rows, width = panel.shape
    blocks = rows // edge
    grid_spec = pltpu.PrefetchScalarGridSpec(
        num_scalar_prefetch=3,
        grid=(slots,),
        in_specs=[
            pl.BlockSpec((1, edge, edge), lambda s, ids, cnt, flag: (jnp.minimum(s, cnt[0] - 1), 0, 0)),
            pl.BlockSpec((rows, width), lambda s, ids, cnt, flag: (0, 0)),
        ],
        out_specs=pl.BlockSpec((blocks, edge + EXTRA, width), lambda s, ids, cnt, flag: (0, 0, 0)),
    )
    flops = slots * edge * edge * width * 2 * 3
    return pl.pallas_call(
        _tile_kernel,
        grid_spec=grid_spec,
        out_shape=jax.ShapeDtypeStruct((blocks, edge + EXTRA, width), jnp.float32),
        compiler_params=pltpu.CompilerParams(
            dimension_semantics=("arbitrary",), vmem_limit_bytes=56 * 1024 * 1024
        ),
        cost_estimate=pl.CostEstimate(
            flops=flops,
            bytes_accessed=tile_set.size * 2 + panel.size * 4 + blocks * (edge + EXTRA) * width * 4,
            transcendentals=0,
        ),
    )(ids, cnt, flag, tile_set, panel)


def shards(features, weight, tile_values, tile_ids, tile_counts):
    tile_set = tile_values[0, 0]
    edge = tile_set.shape[1]
    ids = tile_ids[0, 0].reshape(-1)
    cnt = tile_counts[0, 0].reshape(1)
    flag = (lax.axis_index("row") == lax.axis_index("col")).astype(jnp.int32).reshape(1)
    weighted = jnp.dot(features, weight, precision=lax.Precision.HIGHEST)
    panel = lax.all_gather(weighted, "row", axis=0, tiled=True)
    partial = _panel_products(ids, cnt, flag, tile_set, panel)
    blocks, height, width = partial.shape
    mine = lax.psum_scatter(
        partial.reshape(blocks * height, width), "col", scatter_dimension=0, tiled=True
    )
    degree = 1.0 + mine[edge, :edge]
    inverse_root = lax.rsqrt(degree)
    return jnp.maximum(mine[:edge] * inverse_root[:, None], 0.0)


def solution(mesh):
    in_specs = (
        P(("col", "row"), None),
        P(),
        P("row", "col", None, None, None),
        P("row", "col", None, None),
        P("row", "col"),
    )
    out_specs = P(("row", "col"), None)
    return jax.shard_map(shards, mesh=mesh, in_specs=in_specs, out_specs=out_specs, check_vma=False)
```

```python
import functools

import jax
import jax.numpy as jnp
from jax import lax
from jax.experimental import pallas as pl
from jax.experimental.pallas import tpu as pltpu
from jax.sharding import PartitionSpec as P

EXTRA = 8


def _split3(x):
    hi = x.astype(jnp.bfloat16)
    r1 = x - hi.astype(jnp.float32)
    mid = r1.astype(jnp.bfloat16)
    lo = (r1 - mid.astype(jnp.float32)).astype(jnp.bfloat16)
    return hi, mid, lo


def _tile_kernel(ids_ref, cnt_ref, flag_ref, tile_ref, x_ref, out_ref):
    s = pl.program_id(0)
    edge = tile_ref.shape[1]
    blocks = out_ref.shape[0]
    with_sums = out_ref.shape[1] > edge

    @pl.when(s == 0)
    def _init():
        own = x_ref[...].reshape(blocks, edge, x_ref.shape[1])
        keep = flag_ref[0] != 0
        out_ref[:, :edge, :] = jnp.where(keep, own, jnp.zeros_like(own))
        if with_sums:
            out_ref[:, edge:, :] = jnp.zeros((blocks, EXTRA, out_ref.shape[2]), jnp.float32)

    @pl.when(s < cnt_ref[0])
    def _add():
        i = ids_ref[2 * s]
        j = ids_ref[2 * s + 1]
        tile = tile_ref[0]
        start = pl.multiple_of(j * edge, edge)
        xb = x_ref[pl.ds(start, edge), :]
        hi, mid, lo = _split3(xb)
        prod = jnp.dot(tile, hi, preferred_element_type=jnp.float32)
        prod += jnp.dot(tile, mid, preferred_element_type=jnp.float32)
        prod += jnp.dot(tile, lo, preferred_element_type=jnp.float32)
        out_ref[i, :edge, :] += prod
        if with_sums:
            first = (lax.broadcasted_iota(jnp.int32, (EXTRA, edge), 0) == 0).astype(jnp.bfloat16)
            sums = lax.dot_general(
                first, tile, (((1,), (1,)), ((), ())), preferred_element_type=jnp.float32
            )
            out_ref[i, edge:, :edge] += sums


def _panel_products(ids, cnt, flag, tile_set, panel, with_sums):
    slots, edge, _ = tile_set.shape
    rows, width = panel.shape
    blocks = rows // edge
    height = edge + EXTRA if with_sums else edge
    grid_spec = pltpu.PrefetchScalarGridSpec(
        num_scalar_prefetch=3,
        grid=(slots,),
        in_specs=[
            pl.BlockSpec((1, edge, edge), lambda s, ids, cnt, flag: (jnp.minimum(s, cnt[0] - 1), 0, 0)),
            pl.BlockSpec((rows, width), lambda s, ids, cnt, flag: (0, 0)),
        ],
        out_specs=pl.BlockSpec((blocks, height, width), lambda s, ids, cnt, flag: (0, 0, 0)),
    )
    flops = slots * edge * edge * width * 2 * 3
    return pl.pallas_call(
        _tile_kernel,
        grid_spec=grid_spec,
        out_shape=jax.ShapeDtypeStruct((blocks, height, width), jnp.float32),
        compiler_params=pltpu.CompilerParams(
            dimension_semantics=("arbitrary",), vmem_limit_bytes=56 * 1024 * 1024
        ),
        cost_estimate=pl.CostEstimate(
            flops=flops,
            bytes_accessed=tile_set.size * 2 + panel.size * 4 + blocks * height * width * 4,
            transcendentals=0,
        ),
    )(ids, cnt, flag, tile_set, panel)


def _reduce_over_col(partial, cols):
    chips = cols // 2
    c = lax.axis_index("col")
    z = c // 2
    core = c % 2
    step = 1 - 2 * core
    pairs = partial.reshape((chips, 2) + partial.shape[1:])
    mine = lax.dynamic_index_in_dim(pairs, core, axis=1, keepdims=False)
    theirs = lax.dynamic_index_in_dim(pairs, 1 - core, axis=1, keepdims=False)
    swap = [(a, a ^ 1) for a in range(cols)]
    held = mine + lax.ppermute(theirs, "col", swap)
    ring = [(2 * k, 2 * ((k + 1) % chips)) for k in range(chips)]
    ring += [(2 * k + 1, 2 * ((k - 1) % chips) + 1) for k in range(chips)]
    acc = lax.dynamic_index_in_dim(held, (z - step) % chips, axis=0, keepdims=False)
    for k in range(chips - 1):
        got = lax.ppermute(acc, "col", ring)
        acc = got + lax.dynamic_index_in_dim(held, (z - step * (k + 2)) % chips, axis=0, keepdims=False)
    return acc


def _shards(chunks, features, weight, tile_values, tile_ids, tile_counts):
    tile_set = tile_values[0, 0]
    edge = tile_set.shape[1]
    ids = tile_ids[0, 0].reshape(-1)
    cnt = tile_counts[0, 0].reshape(1)
    flag = (lax.axis_index("row") == lax.axis_index("col")).astype(jnp.int32).reshape(1)
    cols = lax.axis_size("col")
    width = weight.shape[1]
    part = width // chunks
    outs = []
    degree = None
    for k in range(chunks):
        weighted = jnp.dot(
            features, weight[:, k * part:(k + 1) * part], precision=lax.Precision.HIGHEST
        )
        panel = lax.all_gather(weighted, "row", axis=0, tiled=True)
        partial = _panel_products(ids, cnt, flag, tile_set, panel, k == 0)
        mine = _reduce_over_col(partial, cols)
        if k == 0:
            degree = 1.0 + mine[edge, :edge]
        outs.append(mine[:edge])
    inverse_root = lax.rsqrt(degree)
    return jnp.maximum(jnp.concatenate(outs, axis=1) * inverse_root[:, None], 0.0)


def solution(mesh, chunks=2):
    in_specs = (
        P(("col", "row"), None),
        P(),
        P("row", "col", None, None, None),
        P("row", "col", None, None),
        P("row", "col"),
    )
    out_specs = P(("row", "col"), None)
    body = functools.partial(_shards, chunks)
    return jax.shard_map(body, mesh=mesh, in_specs=in_specs, out_specs=out_specs, check_vma=False)
```

```python
import functools

import jax
import jax.numpy as jnp
from jax import lax
from jax.experimental import pallas as pl
from jax.experimental.pallas import tpu as pltpu
from jax.sharding import PartitionSpec as P

EXTRA = 8


def _split3(x):
    hi = x.astype(jnp.bfloat16)
    r1 = x - hi.astype(jnp.float32)
    mid = r1.astype(jnp.bfloat16)
    lo = (r1 - mid.astype(jnp.float32)).astype(jnp.bfloat16)
    return hi, mid, lo


def _tile_kernel(ids_ref, cnt_ref, flag_ref, tile_ref, x_ref, out_ref):
    s = pl.program_id(0)
    edge = tile_ref.shape[1]
    blocks = out_ref.shape[0]
    with_sums = out_ref.shape[1] > edge

    @pl.when(s == 0)
    def _init():
        own = x_ref[...].reshape(blocks, edge, x_ref.shape[1])
        keep = flag_ref[0] != 0
        out_ref[:, :edge, :] = jnp.where(keep, own, jnp.zeros_like(own))
        if with_sums:
            out_ref[:, edge:, :] = jnp.zeros((blocks, EXTRA, out_ref.shape[2]), jnp.float32)

    @pl.when(s < cnt_ref[0])
    def _add():
        i = ids_ref[2 * s]
        j = ids_ref[2 * s + 1]
        tile = tile_ref[0]
        start = pl.multiple_of(j * edge, edge)
        xb = x_ref[pl.ds(start, edge), :]
        hi, mid, lo = _split3(xb)
        prod = jnp.dot(tile, hi, preferred_element_type=jnp.float32)
        prod += jnp.dot(tile, mid, preferred_element_type=jnp.float32)
        prod += jnp.dot(tile, lo, preferred_element_type=jnp.float32)
        out_ref[i, :edge, :] += prod
        if with_sums:
            first = (lax.broadcasted_iota(jnp.int32, (EXTRA, edge), 0) == 0).astype(jnp.bfloat16)
            sums = lax.dot_general(
                first, tile, (((1,), (1,)), ((), ())), preferred_element_type=jnp.float32
            )
            out_ref[i, edge:, :edge] += sums


def _panel_products(ids, cnt, flag, tile_set, panel, with_sums):
    slots, edge, _ = tile_set.shape
    rows, width = panel.shape
    blocks = rows // edge
    height = edge + EXTRA if with_sums else edge
    grid_spec = pltpu.PrefetchScalarGridSpec(
        num_scalar_prefetch=3,
        grid=(slots,),
        in_specs=[
            pl.BlockSpec((1, edge, edge), lambda s, ids, cnt, flag: (jnp.minimum(s, cnt[0] - 1), 0, 0)),
            pl.BlockSpec((rows, width), lambda s, ids, cnt, flag: (0, 0)),
        ],
        out_specs=pl.BlockSpec((blocks, height, width), lambda s, ids, cnt, flag: (0, 0, 0)),
    )
    flops = slots * edge * edge * width * 2 * 3
    return pl.pallas_call(
        _tile_kernel,
        grid_spec=grid_spec,
        out_shape=jax.ShapeDtypeStruct((blocks, height, width), jnp.float32),
        compiler_params=pltpu.CompilerParams(
            dimension_semantics=("arbitrary",), vmem_limit_bytes=56 * 1024 * 1024
        ),
        cost_estimate=pl.CostEstimate(
            flops=flops,
            bytes_accessed=tile_set.size * 2 + panel.size * 4 + blocks * height * width * 4,
            transcendentals=0,
        ),
    )(ids, cnt, flag, tile_set, panel)


def _reduce_over_col(partial, cols):
    chips = cols // 2
    c = lax.axis_index("col")
    z = c // 2
    core = c % 2
    step = 1 - 2 * core
    pairs = partial.reshape((chips, 2) + partial.shape[1:])
    mine = lax.dynamic_index_in_dim(pairs, core, axis=1, keepdims=False)
    theirs = lax.dynamic_index_in_dim(pairs, 1 - core, axis=1, keepdims=False)
    swap = [(a, a ^ 1) for a in range(cols)]
    held = mine + lax.ppermute(theirs, "col", swap)
    ring = [(2 * k, 2 * ((k + 1) % chips)) for k in range(chips)]
    ring += [(2 * k + 1, 2 * ((k - 1) % chips) + 1) for k in range(chips)]
    acc = lax.dynamic_index_in_dim(held, (z - step) % chips, axis=0, keepdims=False)
    for k in range(chips - 1):
        got = lax.ppermute(acc, "col", ring)
        acc = got + lax.dynamic_index_in_dim(held, (z - step * (k + 2)) % chips, axis=0, keepdims=False)
    return acc


def _shards(chunks, features, weight, tile_values, tile_ids, tile_counts):
    tile_set = tile_values[0, 0]
    edge = tile_set.shape[1]
    ids = tile_ids[0, 0].reshape(-1)
    cnt = tile_counts[0, 0].reshape(1)
    flag = (lax.axis_index("row") == lax.axis_index("col")).astype(jnp.int32).reshape(1)
    cols = lax.axis_size("col")
    width = weight.shape[1]
    part = width // chunks
    outs = []
    degree = None
    for k in range(chunks):
        weighted = jnp.dot(
            features, weight[:, k * part:(k + 1) * part], precision=lax.Precision.HIGHEST
        )
        panel = lax.all_gather(weighted, "row", axis=0, tiled=True)
        partial = _panel_products(ids, cnt, flag, tile_set, panel, k == 0)
        mine = _reduce_over_col(partial, cols)
        if k == 0:
            degree = 1.0 + mine[edge, :edge]
        outs.append(mine[:edge])
    inverse_root = lax.rsqrt(degree)
    return jnp.maximum(jnp.concatenate(outs, axis=1) * inverse_root[:, None], 0.0)


def solution(mesh, chunks=1):
    in_specs = (
        P(("col", "row"), None),
        P(),
        P("row", "col", None, None, None),
        P("row", "col", None, None),
        P("row", "col"),
    )
    out_specs = P(("row", "col"), None)
    body = functools.partial(_shards, chunks)
    return jax.shard_map(body, mesh=mesh, in_specs=in_specs, out_specs=out_specs, check_vma=False)
```

```python
import jax
import jax.numpy as jnp
from jax import lax
from jax.experimental import pallas as pl
from jax.experimental.pallas import tpu as pltpu
from jax.sharding import PartitionSpec as P

EXTRA = 8


def _split2(x):
    hi = x.astype(jnp.bfloat16)
    lo = (x - hi.astype(jnp.float32)).astype(jnp.bfloat16)
    return hi, lo


def _tile_kernel(ids_ref, cnt_ref, flag_ref, tile_ref, x_ref, out_ref):
    s = pl.program_id(0)
    edge = tile_ref.shape[1]
    blocks = out_ref.shape[0]

    @pl.when(s == 0)
    def _init():
        own = x_ref[...].reshape(blocks, edge, x_ref.shape[1])
        keep = flag_ref[0] != 0
        out_ref[:, :edge, :] = jnp.where(keep, own, jnp.zeros_like(own))
        out_ref[:, edge:, :] = jnp.zeros((blocks, EXTRA, out_ref.shape[2]), jnp.float32)

    @pl.when(s < cnt_ref[0])
    def _add():
        i = ids_ref[2 * s]
        j = ids_ref[2 * s + 1]
        tile = tile_ref[0]
        start = pl.multiple_of(j * edge, edge)
        xb = x_ref[pl.ds(start, edge), :]
        hi, lo = _split2(xb)
        prod = jnp.dot(tile, hi, preferred_element_type=jnp.float32)
        prod += jnp.dot(tile, lo, preferred_element_type=jnp.float32)
        out_ref[i, :edge, :] += prod
        first = (lax.broadcasted_iota(jnp.int32, (EXTRA, edge), 0) == 0).astype(jnp.bfloat16)
        sums = lax.dot_general(
            first, tile, (((1,), (1,)), ((), ())), preferred_element_type=jnp.float32
        )
        out_ref[i, edge:, :edge] += sums


def _panel_products(ids, cnt, flag, tile_set, panel):
    slots, edge, _ = tile_set.shape
    rows, width = panel.shape
    blocks = rows // edge
    grid_spec = pltpu.PrefetchScalarGridSpec(
        num_scalar_prefetch=3,
        grid=(slots,),
        in_specs=[
            pl.BlockSpec((1, edge, edge), lambda s, ids, cnt, flag: (jnp.minimum(s, cnt[0] - 1), 0, 0)),
            pl.BlockSpec((rows, width), lambda s, ids, cnt, flag: (0, 0)),
        ],
        out_specs=pl.BlockSpec((blocks, edge + EXTRA, width), lambda s, ids, cnt, flag: (0, 0, 0)),
    )
    flops = slots * edge * edge * width * 2 * 2
    return pl.pallas_call(
        _tile_kernel,
        grid_spec=grid_spec,
        out_shape=jax.ShapeDtypeStruct((blocks, edge + EXTRA, width), jnp.float32),
        compiler_params=pltpu.CompilerParams(
            dimension_semantics=("arbitrary",), vmem_limit_bytes=56 * 1024 * 1024
        ),
        cost_estimate=pl.CostEstimate(
            flops=flops,
            bytes_accessed=tile_set.size * 2 + panel.size * 4 + blocks * (edge + EXTRA) * width * 4,
            transcendentals=0,
        ),
    )(ids, cnt, flag, tile_set, panel)


def shards(features, weight, tile_values, tile_ids, tile_counts):
    tile_set = tile_values[0, 0]
    edge = tile_set.shape[1]
    ids = tile_ids[0, 0].reshape(-1)
    cnt = tile_counts[0, 0].reshape(1)
    flag = (lax.axis_index("row") == lax.axis_index("col")).astype(jnp.int32).reshape(1)
    weighted = jnp.dot(features, weight, precision=lax.Precision.HIGH)
    panel = lax.all_gather(weighted, "row", axis=0, tiled=True)
    partial = _panel_products(ids, cnt, flag, tile_set, panel)
    blocks, height, width = partial.shape
    mine = lax.psum_scatter(
        partial.reshape(blocks * height, width), "col", scatter_dimension=0, tiled=True
    )
    degree = 1.0 + mine[edge, :edge]
    inverse_root = lax.rsqrt(degree)
    return jnp.maximum(mine[:edge] * inverse_root[:, None], 0.0)


def solution(mesh):
    in_specs = (
        P(("col", "row"), None),
        P(),
        P("row", "col", None, None, None),
        P("row", "col", None, None),
        P("row", "col"),
    )
    out_specs = P(("row", "col"), None)
    return jax.shard_map(shards, mesh=mesh, in_specs=in_specs, out_specs=out_specs, check_vma=False)
```

```python
import jax
import jax.numpy as jnp
from jax import lax
from jax.experimental import pallas as pl
from jax.experimental.pallas import tpu as pltpu
from jax.sharding import PartitionSpec as P

EXTRA = 8


def _tile_kernel(ids_ref, cnt_ref, flag_ref, tile_ref, x_ref, extra_ref, out_ref):
    s = pl.program_id(0)
    edge = tile_ref.shape[1]
    blocks = out_ref.shape[0]

    @pl.when(s == 0)
    def _init():
        keep = flag_ref[0] != 0
        for b in range(blocks):
            hi = x_ref[2 * b * edge:(2 * b + 1) * edge, :].astype(jnp.float32)
            lo = x_ref[(2 * b + 1) * edge:(2 * b + 2) * edge, :].astype(jnp.float32)
            own = hi + lo
            out_ref[b, :edge, :] = jnp.where(keep, own, jnp.zeros_like(own))
        out_ref[:, edge:, :] = extra_ref[...]

    @pl.when(s < cnt_ref[0])
    def _add():
        i = ids_ref[2 * s]
        j = ids_ref[2 * s + 1]
        start = pl.multiple_of(j * 2 * edge, 2 * edge)
        pair = x_ref[pl.ds(start, 2 * edge), :]
        out_ref[i, :edge, :] += jnp.dot(tile_ref[0], pair, preferred_element_type=jnp.float32)


def _panel_products(ids, cnt, flag, doubled, panel, extra):
    slots, edge, _ = doubled.shape
    rows, width = panel.shape
    blocks = rows // (2 * edge)
    height = edge + extra.shape[1]
    grid_spec = pltpu.PrefetchScalarGridSpec(
        num_scalar_prefetch=3,
        grid=(slots,),
        in_specs=[
            pl.BlockSpec((1, edge, 2 * edge), lambda s, ids, cnt, flag: (jnp.minimum(s, cnt[0] - 1), 0, 0)),
            pl.BlockSpec((rows, width), lambda s, ids, cnt, flag: (0, 0)),
            pl.BlockSpec(extra.shape, lambda s, ids, cnt, flag: (0, 0, 0)),
        ],
        out_specs=pl.BlockSpec((blocks, height, width), lambda s, ids, cnt, flag: (0, 0, 0)),
    )
    flops = slots * edge * 2 * edge * width * 2
    return pl.pallas_call(
        _tile_kernel,
        grid_spec=grid_spec,
        out_shape=jax.ShapeDtypeStruct((blocks, height, width), jnp.float32),
        compiler_params=pltpu.CompilerParams(
            dimension_semantics=("arbitrary",), vmem_limit_bytes=56 * 1024 * 1024
        ),
        cost_estimate=pl.CostEstimate(
            flops=flops,
            bytes_accessed=doubled.size * 2 + panel.size * 2 + blocks * height * width * 4,
            transcendentals=0,
        ),
    )(ids, cnt, flag, doubled, panel, extra)


def shards(features, weight, tile_values, tile_ids, tile_counts):
    tile_set = tile_values[0, 0]
    slots, edge, _ = tile_set.shape
    slot_ids = tile_ids[0, 0]
    ids = slot_ids.reshape(-1)
    live_count = tile_counts[0, 0]
    cnt = live_count.reshape(1)
    flag = (lax.axis_index("row") == lax.axis_index("col")).astype(jnp.int32).reshape(1)
    weighted = jnp.dot(features, weight, precision=lax.Precision.HIGH)
    rounded = lax.reduce_precision(weighted, exponent_bits=8, mantissa_bits=7)
    hi = rounded.astype(jnp.bfloat16)
    lo = (weighted - rounded).astype(jnp.bfloat16)
    panel = lax.all_gather(jnp.concatenate([hi, lo], axis=0), "row", axis=0, tiled=True)
    blocks = panel.shape[0] // (2 * edge)
    width = panel.shape[1]
    doubled = jnp.concatenate([tile_set, tile_set], axis=2)
    is_live = (jnp.arange(slots) < live_count).astype(jnp.float32)
    placement = (slot_ids[:, 0][:, None] == jnp.arange(blocks)[None, :]).astype(jnp.float32)
    placement = placement * is_live[:, None]
    tile_sums = jnp.sum(tile_set, axis=2, dtype=jnp.float32)
    row_sums = jnp.dot(placement.T, tile_sums, precision=lax.Precision.HIGHEST)
    extra = jnp.zeros((blocks, EXTRA, width), jnp.float32).at[:, 0, :edge].set(row_sums)
    partial = _panel_products(ids, cnt, flag, doubled, panel, extra)
    _, height, _ = partial.shape
    mine = lax.psum_scatter(
        partial.reshape(blocks * height, width), "col", scatter_dimension=0, tiled=True
    )
    degree = 1.0 + mine[edge, :edge]
    inverse_root = lax.rsqrt(degree)
    return jnp.maximum(mine[:edge] * inverse_root[:, None], 0.0)


def solution(mesh):
    in_specs = (
        P(("col", "row"), None),
        P(),
        P("row", "col", None, None, None),
        P("row", "col", None, None),
        P("row", "col"),
    )
    out_specs = P(("row", "col"), None)
    return jax.shard_map(shards, mesh=mesh, in_specs=in_specs, out_specs=out_specs, check_vma=False)
```

```python
import jax
import jax.numpy as jnp
from jax import lax
from jax.experimental import pallas as pl
from jax.experimental.pallas import tpu as pltpu
from jax.sharding import PartitionSpec as P

EXTRA = 8


def _tile_kernel(ids_ref, cnt_ref, flag_ref, tile_ref, x_ref, extra_ref, panel_ref, out_ref, own_ref, sem):
    s = pl.program_id(0)
    edge = tile_ref.shape[1]
    blocks = out_ref.shape[0]

    @pl.when(s == 0)
    def _init():
        out_ref[:, edge:, :] = extra_ref[...]

        @pl.when(flag_ref[0] != 0)
        def _diagonal():
            copy = pltpu.make_async_copy(panel_ref, own_ref, sem)
            copy.start()
            copy.wait()
            for b in range(blocks):
                own = own_ref[b, :edge, :].astype(jnp.float32) + own_ref[b, edge:, :].astype(jnp.float32)
                out_ref[b, :edge, :] = own

        @pl.when(flag_ref[0] == 0)
        def _elsewhere():
            out_ref[:, :edge, :] = jnp.zeros((blocks, edge, out_ref.shape[2]), jnp.float32)

    @pl.when(s < cnt_ref[0])
    def _add():
        i = ids_ref[2 * s]
        out_ref[i, :edge, :] += jnp.dot(tile_ref[0], x_ref[0], preferred_element_type=jnp.float32)


def _live_slot(s, cnt):
    return jnp.minimum(s, cnt[0] - 1)


def _panel_products(ids, cnt, flag, doubled, panel, extra):
    slots, edge, _ = doubled.shape
    blocks, pair, width = panel.shape
    height = edge + extra.shape[1]
    grid_spec = pltpu.PrefetchScalarGridSpec(
        num_scalar_prefetch=3,
        grid=(slots,),
        in_specs=[
            pl.BlockSpec((1, edge, 2 * edge), lambda s, ids, cnt, flag: (_live_slot(s, cnt), 0, 0)),
            pl.BlockSpec(
                (1, pair, width),
                lambda s, ids, cnt, flag: (ids[2 * _live_slot(s, cnt) + 1], 0, 0),
            ),
            pl.BlockSpec(extra.shape, lambda s, ids, cnt, flag: (0, 0, 0)),
            pl.BlockSpec(memory_space=pl.ANY),
        ],
        out_specs=pl.BlockSpec((blocks, height, width), lambda s, ids, cnt, flag: (0, 0, 0)),
        scratch_shapes=[
            pltpu.VMEM((blocks, pair, width), panel.dtype),
            pltpu.SemaphoreType.DMA,
        ],
    )
    flops = slots * edge * 2 * edge * width * 2
    return pl.pallas_call(
        _tile_kernel,
        grid_spec=grid_spec,
        out_shape=jax.ShapeDtypeStruct((blocks, height, width), jnp.float32),
        compiler_params=pltpu.CompilerParams(
            dimension_semantics=("arbitrary",), vmem_limit_bytes=56 * 1024 * 1024
        ),
        cost_estimate=pl.CostEstimate(
            flops=flops,
            bytes_accessed=doubled.size * 2 + panel.size * 2 + blocks * height * width * 4,
            transcendentals=0,
        ),
    )(ids, cnt, flag, doubled, panel, extra, panel)


def shards(features, weight, tile_values, tile_ids, tile_counts):
    tile_set = tile_values[0, 0]
    slots, edge, _ = tile_set.shape
    slot_ids = tile_ids[0, 0]
    ids = slot_ids.reshape(-1)
    live_count = tile_counts[0, 0]
    cnt = live_count.reshape(1)
    flag = (lax.axis_index("row") == lax.axis_index("col")).astype(jnp.int32).reshape(1)
    weighted = jnp.dot(features, weight, precision=lax.Precision.HIGH)
    rounded = lax.reduce_precision(weighted, exponent_bits=8, mantissa_bits=7)
    hi = rounded.astype(jnp.bfloat16)
    lo = (weighted - rounded).astype(jnp.bfloat16)
    panel = lax.all_gather(jnp.concatenate([hi, lo], axis=0), "row", axis=0, tiled=True)
    blocks = panel.shape[0] // (2 * edge)
    width = panel.shape[1]
    doubled = jnp.concatenate([tile_set, tile_set], axis=2)
    is_live = (jnp.arange(slots) < live_count).astype(jnp.float32)
    placement = (slot_ids[:, 0][:, None] == jnp.arange(blocks)[None, :]).astype(jnp.float32)
    placement = placement * is_live[:, None]
    tile_sums = jnp.sum(tile_set, axis=2, dtype=jnp.float32)
    row_sums = jnp.dot(placement.T, tile_sums, precision=lax.Precision.HIGHEST)
    extra = jnp.zeros((blocks, EXTRA, width), jnp.float32).at[:, 0, :edge].set(row_sums)
    partial = _panel_products(ids, cnt, flag, doubled, panel.reshape(blocks, 2 * edge, width), extra)
    _, height, _ = partial.shape
    mine = lax.psum_scatter(
        partial.reshape(blocks * height, width), "col", scatter_dimension=0, tiled=True
    )
    degree = 1.0 + mine[edge, :edge]
    inverse_root = lax.rsqrt(degree)
    return jnp.maximum(mine[:edge] * inverse_root[:, None], 0.0)


def solution(mesh):
    in_specs = (
        P(("col", "row"), None),
        P(),
        P("row", "col", None, None, None),
        P("row", "col", None, None),
        P("row", "col"),
    )
    out_specs = P(("row", "col"), None)
    return jax.shard_map(shards, mesh=mesh, in_specs=in_specs, out_specs=out_specs, check_vma=False)
```

```python
import jax
import jax.numpy as jnp
from jax import lax
from jax.experimental import pallas as pl
from jax.experimental.pallas import tpu as pltpu
from jax.sharding import PartitionSpec as P

EXTRA = 8


def _tile_kernel(ids_ref, cnt_ref, flag_ref, tile_ref, x_ref, extra_ref, panel_ref, out_ref, own_ref, sem):
    s = pl.program_id(0)
    blocks, height, edge = out_ref.shape
    width = x_ref.shape[1] // 2

    @pl.when(s == 0)
    def _init():
        out_ref[:, width:, :] = extra_ref[...]

        @pl.when(flag_ref[0] != 0)
        def _diagonal():
            copy = pltpu.make_async_copy(panel_ref, own_ref, sem)
            copy.start()
            copy.wait()
            for b in range(blocks):
                own = own_ref[b, :width, :].astype(jnp.float32) + own_ref[b, width:, :].astype(jnp.float32)
                out_ref[b, :width, :] = own

        @pl.when(flag_ref[0] == 0)
        def _elsewhere():
            out_ref[:, :width, :] = jnp.zeros((blocks, width, edge), jnp.float32)

    @pl.when(s < cnt_ref[0])
    def _add():
        i = ids_ref[2 * s]
        both = jnp.dot(x_ref[0], tile_ref[0], preferred_element_type=jnp.float32)
        out_ref[i, :width, :] += both[:width] + both[width:]


def _live_slot(s, cnt):
    return jnp.minimum(s, cnt[0] - 1)


def _panel_products(ids, cnt, flag, turned, panel, extra):
    slots, edge, _ = turned.shape
    blocks, pair, _ = panel.shape
    width = pair // 2
    height = width + extra.shape[1]
    grid_spec = pltpu.PrefetchScalarGridSpec(
        num_scalar_prefetch=3,
        grid=(slots,),
        in_specs=[
            pl.BlockSpec((1, edge, edge), lambda s, ids, cnt, flag: (_live_slot(s, cnt), 0, 0)),
            pl.BlockSpec(
                (1, pair, edge),
                lambda s, ids, cnt, flag: (ids[2 * _live_slot(s, cnt) + 1], 0, 0),
            ),
            pl.BlockSpec(extra.shape, lambda s, ids, cnt, flag: (0, 0, 0)),
            pl.BlockSpec(memory_space=pl.ANY),
        ],
        out_specs=pl.BlockSpec((blocks, height, edge), lambda s, ids, cnt, flag: (0, 0, 0)),
        scratch_shapes=[
            pltpu.VMEM((blocks, pair, edge), panel.dtype),
            pltpu.SemaphoreType.DMA,
        ],
    )
    flops = slots * pair * edge * edge * 2
    return pl.pallas_call(
        _tile_kernel,
        grid_spec=grid_spec,
        out_shape=jax.ShapeDtypeStruct((blocks, height, edge), jnp.float32),
        compiler_params=pltpu.CompilerParams(
            dimension_semantics=("arbitrary",), vmem_limit_bytes=56 * 1024 * 1024
        ),
        cost_estimate=pl.CostEstimate(
            flops=flops,
            bytes_accessed=turned.size * 2 + panel.size * 2 + blocks * height * edge * 4,
            transcendentals=0,
        ),
    )(ids, cnt, flag, turned, panel, extra, panel)


def shards(features, weight, tile_values, tile_ids, tile_counts):
    tile_set = tile_values[0, 0]
    slots, edge, _ = tile_set.shape
    slot_ids = tile_ids[0, 0]
    ids = slot_ids.reshape(-1)
    live_count = tile_counts[0, 0]
    cnt = live_count.reshape(1)
    flag = (lax.axis_index("row") == lax.axis_index("col")).astype(jnp.int32).reshape(1)
    turned_w = lax.dot_general(
        weight, features, (((0,), (1,)), ((), ())), precision=lax.Precision.HIGH
    )
    rounded = lax.reduce_precision(turned_w, exponent_bits=8, mantissa_bits=7)
    hi = rounded.astype(jnp.bfloat16)
    lo = (turned_w - rounded).astype(jnp.bfloat16)
    stacked = jnp.concatenate([hi, lo], axis=0)[None]
    panel = lax.all_gather(stacked, "row", axis=0, tiled=True)
    blocks, pair, _ = panel.shape
    width = pair // 2
    turned = jnp.swapaxes(tile_set, 1, 2)
    is_live = (jnp.arange(slots) < live_count).astype(jnp.float32)
    placement = (slot_ids[:, 0][:, None] == jnp.arange(blocks)[None, :]).astype(jnp.float32)
    placement = placement * is_live[:, None]
    tile_sums = jnp.sum(tile_set, axis=2, dtype=jnp.float32)
    row_sums = jnp.dot(placement.T, tile_sums, precision=lax.Precision.HIGHEST)
    extra = jnp.zeros((blocks, EXTRA, edge), jnp.float32).at[:, 0, :].set(row_sums)
    partial = _panel_products(ids, cnt, flag, turned, panel, extra)
    _, height, _ = partial.shape
    mine = lax.psum_scatter(
        partial.reshape(blocks * height, edge), "col", scatter_dimension=0, tiled=True
    )
    degree = 1.0 + mine[width]
    inverse_root = lax.rsqrt(degree)
    return jnp.maximum(mine[:width].T * inverse_root[:, None], 0.0)


def solution(mesh):
    in_specs = (
        P(("col", "row"), None),
        P(),
        P("row", "col", None, None, None),
        P("row", "col", None, None),
        P("row", "col"),
    )
    out_specs = P(("row", "col"), None)
    return jax.shard_map(shards, mesh=mesh, in_specs=in_specs, out_specs=out_specs, check_vma=False)
```

```python
import jax
import jax.numpy as jnp
from jax import lax
from jax.experimental import pallas as pl
from jax.experimental.pallas import tpu as pltpu
from jax.sharding import PartitionSpec as P

EXTRA = 8


def _tile_kernel(ids_ref, cnt_ref, flag_ref, tile_ref, x_ref, extra_ref, out_ref):
    blocks, height, edge = out_ref.shape
    width = x_ref.shape[1] // 2
    out_ref[:, width:, :] = extra_ref[...]

    @pl.when(flag_ref[0] != 0)
    def _diagonal():
        for b in range(blocks):
            own = x_ref[b, :width, :].astype(jnp.float32) + x_ref[b, width:, :].astype(jnp.float32)
            out_ref[b, :width, :] = own

    @pl.when(flag_ref[0] == 0)
    def _elsewhere():
        out_ref[:, :width, :] = jnp.zeros((blocks, width, edge), jnp.float32)

    def one_slot(s, carry):
        i = ids_ref[2 * s]
        j = ids_ref[2 * s + 1]
        both = jnp.dot(x_ref[j], tile_ref[s], preferred_element_type=jnp.float32)
        out_ref[i, :width, :] += both[:width] + both[width:]
        return carry

    lax.fori_loop(0, cnt_ref[0], one_slot, 0)


def _panel_products(ids, cnt, flag, turned, panel, extra):
    slots, edge, _ = turned.shape
    blocks, pair, _ = panel.shape
    width = pair // 2
    height = width + extra.shape[1]
    smem = pl.BlockSpec(memory_space=pltpu.SMEM)
    vmem = pl.BlockSpec(memory_space=pltpu.VMEM)
    flops = slots * pair * edge * edge * 2
    return pl.pallas_call(
        _tile_kernel,
        in_specs=[smem, smem, smem, vmem, vmem, vmem],
        out_specs=vmem,
        out_shape=jax.ShapeDtypeStruct((blocks, height, edge), jnp.float32),
        compiler_params=pltpu.CompilerParams(vmem_limit_bytes=56 * 1024 * 1024),
        cost_estimate=pl.CostEstimate(
            flops=flops,
            bytes_accessed=turned.size * 2 + panel.size * 2 + blocks * height * edge * 4,
            transcendentals=0,
        ),
    )(ids, cnt, flag, turned, panel, extra)


def shards(features, weight, tile_values, tile_ids, tile_counts):
    tile_set = tile_values[0, 0]
    slots, edge, _ = tile_set.shape
    slot_ids = tile_ids[0, 0]
    ids = slot_ids.reshape(-1)
    live_count = tile_counts[0, 0]
    cnt = live_count.reshape(1)
    flag = (lax.axis_index("row") == lax.axis_index("col")).astype(jnp.int32).reshape(1)
    turned_w = lax.dot_general(
        weight, features, (((0,), (1,)), ((), ())), precision=lax.Precision.HIGH
    )
    rounded = lax.reduce_precision(turned_w, exponent_bits=8, mantissa_bits=7)
    hi = rounded.astype(jnp.bfloat16)
    lo = (turned_w - rounded).astype(jnp.bfloat16)
    stacked = jnp.concatenate([hi, lo], axis=0)[None]
    panel = lax.all_gather(stacked, "row", axis=0, tiled=True)
    blocks, pair, _ = panel.shape
    width = pair // 2
    turned = jnp.swapaxes(tile_set, 1, 2)
    is_live = (jnp.arange(slots) < live_count).astype(jnp.float32)
    placement = (slot_ids[:, 0][:, None] == jnp.arange(blocks)[None, :]).astype(jnp.float32)
    placement = placement * is_live[:, None]
    tile_sums = jnp.sum(tile_set, axis=2, dtype=jnp.float32)
    row_sums = jnp.dot(placement.T, tile_sums, precision=lax.Precision.HIGHEST)
    extra = jnp.zeros((blocks, EXTRA, edge), jnp.float32).at[:, 0, :].set(row_sums)
    partial = _panel_products(ids, cnt, flag, turned, panel, extra)
    _, height, _ = partial.shape
    mine = lax.psum_scatter(
        partial.reshape(blocks * height, edge), "col", scatter_dimension=0, tiled=True
    )
    degree = 1.0 + mine[width]
    inverse_root = lax.rsqrt(degree)
    return jnp.maximum(mine[:width].T * inverse_root[:, None], 0.0)


def solution(mesh):
    in_specs = (
        P(("col", "row"), None),
        P(),
        P("row", "col", None, None, None),
        P("row", "col", None, None),
        P("row", "col"),
    )
    out_specs = P(("row", "col"), None)
    return jax.shard_map(shards, mesh=mesh, in_specs=in_specs, out_specs=out_specs, check_vma=False)
```

```python
import jax
import jax.numpy as jnp
from jax import lax
from jax.experimental import pallas as pl
from jax.experimental.pallas import tpu as pltpu
from jax.sharding import PartitionSpec as P

EXTRA = 8


def _tile_kernel(ids_ref, cnt_ref, pos_ref, tile_ref, xa_ref, xb_ref, extra_ref, out_ref):
    blocks, height, edge = out_ref.shape
    part = xa_ref.shape[1] // 2
    side = pos_ref[2]
    x = pos_ref[0]
    y = pos_ref[1]
    if height > 2 * part:
        out_ref[:, 2 * part:, :] = extra_ref[...]

    def where_of(j):
        dx = (j % side - x + side) % side
        dy = (j // side - y + side) % side
        return dy * side + dx, dx * side + dy

    def add_block(i, a_idx, b_idx, tile):
        for ref, at, lo in ((xa_ref, a_idx, 0), (xb_ref, b_idx, part)):
            both = jnp.dot(ref[at], tile, preferred_element_type=jnp.float32)
            out_ref[i, lo:lo + part, :] += both[:part] + both[part:]

    out_ref[:, :2 * part, :] = jnp.zeros((blocks, 2 * part, edge), jnp.float32)

    @pl.when(pos_ref[3] != 0)
    def _diagonal():
        for b in range(blocks):
            a_idx, b_idx = where_of(b)
            for ref, at, lo in ((xa_ref, a_idx, 0), (xb_ref, b_idx, part)):
                own = ref[at, :part, :].astype(jnp.float32) + ref[at, part:, :].astype(jnp.float32)
                out_ref[b, lo:lo + part, :] = own

    def one_slot(s, carry):
        i = ids_ref[2 * s]
        a_idx, b_idx = where_of(ids_ref[2 * s + 1])
        add_block(i, a_idx, b_idx, tile_ref[s])
        return carry

    lax.fori_loop(0, cnt_ref[0], one_slot, 0)


def _panel_products(ids, cnt, pos, turned, panel_a, panel_b, extra):
    slots, edge, _ = turned.shape
    blocks, pair, _ = panel_a.shape
    part = pair // 2
    height = 2 * part + (extra.shape[1] if extra is not None else 0)
    smem = pl.BlockSpec(memory_space=pltpu.SMEM)
    vmem = pl.BlockSpec(memory_space=pltpu.VMEM)
    if extra is None:
        extra = jnp.zeros((blocks, 8, edge), jnp.float32)
    flops = slots * 2 * pair * edge * edge * 2
    return pl.pallas_call(
        _tile_kernel,
        in_specs=[smem, smem, smem, vmem, vmem, vmem, vmem],
        out_specs=vmem,
        out_shape=jax.ShapeDtypeStruct((blocks, height, edge), jnp.float32),
        compiler_params=pltpu.CompilerParams(vmem_limit_bytes=56 * 1024 * 1024),
        cost_estimate=pl.CostEstimate(
            flops=flops,
            bytes_accessed=turned.size * 2 + 2 * panel_a.size * 2 + blocks * height * edge * 4,
            transcendentals=0,
        ),
    )(ids, cnt, pos, turned, panel_a, panel_b, extra)


def _ring4(unit, plus, minus):
    from_left = lax.ppermute(unit, "row", plus)
    from_right = lax.ppermute(unit, "row", minus)
    half = unit.shape[-2] // 2
    first = lax.ppermute(from_left[..., :half, :], "row", plus)
    second = lax.ppermute(from_right[..., half:, :], "row", minus)
    across = jnp.concatenate([first, second], axis=-2)
    return jnp.stack([unit, from_right, across, from_left])


def _gather_2d(block, side):
    n = side * side

    def shift(dx, dy):
        return [(r, ((r // side + dy) % side) * side + (r % side + dx) % side) for r in range(n)]

    half = block.shape[0] // 2
    quarter = block.shape[0] // 4
    hi, lo = block[:half], block[half:]
    unit_a = jnp.concatenate([hi[:quarter], lo[:quarter]], axis=0)
    unit_b = jnp.concatenate([hi[quarter:], lo[quarter:]], axis=0)
    by_x = _ring4(unit_a, shift(1, 0), shift(-1, 0))
    by_y = _ring4(unit_b, shift(0, 1), shift(0, -1))
    panel_a = _ring4(by_x, shift(0, 1), shift(0, -1))
    panel_b = _ring4(by_y, shift(1, 0), shift(-1, 0))
    rows, width = unit_a.shape
    return panel_a.reshape(n, rows, width), panel_b.reshape(n, rows, width)


def shards(features, weight, tile_values, tile_ids, tile_counts):
    tile_set = tile_values[0, 0]
    slots, edge, _ = tile_set.shape
    slot_ids = tile_ids[0, 0]
    ids = slot_ids.reshape(-1)
    live_count = tile_counts[0, 0]
    cnt = live_count.reshape(1)
    n_row = lax.axis_size("row")
    side = 4
    r = lax.axis_index("row")
    on_diagonal = (r == lax.axis_index("col")).astype(jnp.int32)
    pos = jnp.stack([r % side, r // side, jnp.int32(side), on_diagonal]).astype(jnp.int32)
    turned_w = lax.dot_general(
        weight, features, (((0,), (1,)), ((), ())), precision=lax.Precision.HIGH
    )
    rounded = lax.reduce_precision(turned_w, exponent_bits=8, mantissa_bits=7)
    hi = rounded.astype(jnp.bfloat16)
    lo = (turned_w - rounded).astype(jnp.bfloat16)
    width = hi.shape[0]
    turned = jnp.swapaxes(tile_set, 1, 2)
    blocks = n_row
    is_live = (jnp.arange(slots) < live_count).astype(jnp.float32)
    placement = (slot_ids[:, 0][:, None] == jnp.arange(blocks)[None, :]).astype(jnp.float32)
    placement = placement * is_live[:, None]
    tile_sums = jnp.sum(tile_set, axis=2, dtype=jnp.float32)
    row_sums = jnp.dot(placement.T, tile_sums, precision=lax.Precision.HIGHEST)
    extra = jnp.zeros((blocks, EXTRA, edge), jnp.float32).at[:, 0, :].set(row_sums)
    chunks = 2
    step = width // chunks
    pieces = []
    degree = None
    for k in range(chunks):
        block = jnp.concatenate([hi[k * step:(k + 1) * step], lo[k * step:(k + 1) * step]], axis=0)
        panel_a, panel_b = _gather_2d(block, side)
        partial = _panel_products(ids, cnt, pos, turned, panel_a, panel_b, extra if k == 0 else None)
        _, height, _ = partial.shape
        mine = lax.psum_scatter(
            partial.reshape(blocks * height, edge), "col", scatter_dimension=0, tiled=True
        )
        if k == 0:
            degree = 1.0 + mine[step]
        pieces.append(mine[:step])
    inverse_root = lax.rsqrt(degree)
    return jnp.maximum(jnp.concatenate(pieces, axis=0).T * inverse_root[:, None], 0.0)


def solution(mesh):
    in_specs = (
        P(("col", "row"), None),
        P(),
        P("row", "col", None, None, None),
        P("row", "col", None, None),
        P("row", "col"),
    )
    out_specs = P(("row", "col"), None)
    return jax.shard_map(shards, mesh=mesh, in_specs=in_specs, out_specs=out_specs, check_vma=False)
```

```python
import jax
import jax.numpy as jnp
from jax import lax
from jax.experimental import pallas as pl
from jax.experimental.pallas import tpu as pltpu
from jax.sharding import PartitionSpec as P

EXTRA = 8


def _slot_of(block, blocks):
    return (block % 2) * (blocks // 2) + block // 2


def _tile_kernel(ids_ref, cnt_ref, flag_ref, tile_ref, x_ref, extra_ref, out_ref):
    blocks, height, edge = out_ref.shape
    width = x_ref.shape[1] // 2
    out_ref[:, width:, :] = extra_ref[...]

    @pl.when(flag_ref[0] != 0)
    def _diagonal():
        for b in range(blocks):
            own = x_ref[b, :width, :].astype(jnp.float32) + x_ref[b, width:, :].astype(jnp.float32)
            out_ref[_slot_of(b, blocks), :width, :] = own

    @pl.when(flag_ref[0] == 0)
    def _elsewhere():
        out_ref[:, :width, :] = jnp.zeros((blocks, width, edge), jnp.float32)

    def one_slot(s, carry):
        i = ids_ref[2 * s]
        j = ids_ref[2 * s + 1]
        both = jnp.dot(x_ref[j], tile_ref[s], preferred_element_type=jnp.float32)
        out_ref[i, :width, :] += both[:width] + both[width:]
        return carry

    lax.fori_loop(0, cnt_ref[0], one_slot, 0)


def _panel_products(ids, cnt, flag, turned, panel, extra):
    slots, edge, _ = turned.shape
    blocks, pair, _ = panel.shape
    width = pair // 2
    height = width + extra.shape[1]
    smem = pl.BlockSpec(memory_space=pltpu.SMEM)
    vmem = pl.BlockSpec(memory_space=pltpu.VMEM)
    flops = slots * pair * edge * edge * 2
    return pl.pallas_call(
        _tile_kernel,
        in_specs=[smem, smem, smem, vmem, vmem, vmem],
        out_specs=vmem,
        out_shape=jax.ShapeDtypeStruct((blocks, height, edge), jnp.float32),
        compiler_params=pltpu.CompilerParams(vmem_limit_bytes=56 * 1024 * 1024),
        cost_estimate=pl.CostEstimate(
            flops=flops,
            bytes_accessed=turned.size * 2 + panel.size * 2 + blocks * height * edge * 4,
            transcendentals=0,
        ),
    )(ids, cnt, flag, turned, panel, extra)


def shards(features, weight, tile_values, tile_ids, tile_counts):
    tile_set = tile_values[0, 0]
    slots, edge, _ = tile_set.shape
    slot_ids = tile_ids[0, 0]
    blocks = lax.axis_size("row")
    stored = jnp.stack([_slot_of(slot_ids[:, 0], blocks), slot_ids[:, 1]], axis=1)
    ids = stored.reshape(-1)
    live_count = tile_counts[0, 0]
    cnt = live_count.reshape(1)
    col = lax.axis_index("z") * lax.axis_size("core") + lax.axis_index("core")
    flag = (lax.axis_index("row") == col).astype(jnp.int32).reshape(1)
    turned_w = lax.dot_general(
        weight, features, (((0,), (1,)), ((), ())), precision=lax.Precision.HIGH
    )
    rounded = lax.reduce_precision(turned_w, exponent_bits=8, mantissa_bits=7)
    hi = rounded.astype(jnp.bfloat16)
    lo = (turned_w - rounded).astype(jnp.bfloat16)
    stacked = jnp.concatenate([hi, lo], axis=0)[None]
    panel = lax.all_gather(stacked, "row", axis=0, tiled=True)
    _, pair, _ = panel.shape
    width = pair // 2
    turned = jnp.swapaxes(tile_set, 1, 2)
    is_live = (jnp.arange(slots) < live_count).astype(jnp.float32)
    placement = (slot_ids[:, 0][:, None] == jnp.arange(blocks)[None, :]).astype(jnp.float32)
    placement = placement * is_live[:, None]
    tile_sums = jnp.sum(tile_set, axis=2, dtype=jnp.float32)
    row_sums = jnp.dot(placement.T, tile_sums, precision=lax.Precision.HIGHEST)
    order = _slot_of(jnp.arange(blocks), blocks)
    extra = jnp.zeros((blocks, EXTRA, edge), jnp.float32).at[order, 0, :].set(row_sums)
    partial = _panel_products(ids, cnt, flag, turned, panel, extra)
    _, height, _ = partial.shape
    half = lax.psum_scatter(
        partial.reshape(blocks * height, edge), "core", scatter_dimension=0, tiled=True
    )
    mine = lax.psum_scatter(half, "z", scatter_dimension=0, tiled=True)
    degree = 1.0 + mine[width]
    inverse_root = lax.rsqrt(degree)
    return jnp.maximum(mine[:width].T * inverse_root[:, None], 0.0)


def solution(mesh):
    rows, cols = mesh.devices.shape
    mesh = jax.sharding.Mesh(mesh.devices.reshape(rows, cols // 2, 2), ("row", "z", "core"))
    col = ("z", "core")
    in_specs = (
        P((*col, "row"), None),
        P(),
        P("row", col, None, None, None),
        P("row", col, None, None),
        P("row", col),
    )
    out_specs = P(("row", *col), None)
    return jax.shard_map(shards, mesh=mesh, in_specs=in_specs, out_specs=out_specs, check_vma=False)
```

```python
import jax
import jax.numpy as jnp
from jax import lax
from jax.experimental import pallas as pl
from jax.experimental.pallas import tpu as pltpu
from jax.sharding import PartitionSpec as P

EXTRA = 8


def _tile_kernel(ids_ref, cnt_ref, flag_ref, tile_hbm, x_hbm, extra_ref, out_ref,
                 own_ref, tbuf, xbuf, tsem, xsem, own_sem):
    blocks, height, edge = out_ref.shape
    width = x_hbm.shape[1] // 2
    count = cnt_ref[0]

    def copies(s, slot):
        j = ids_ref[2 * s + 1]
        return (
            pltpu.make_async_copy(tile_hbm.at[s], tbuf.at[slot], tsem.at[slot]),
            pltpu.make_async_copy(x_hbm.at[j], xbuf.at[slot], xsem.at[slot]),
        )

    for c in copies(0, 0):
        c.start()
    out_ref[:, width:, :] = extra_ref[...]

    @pl.when(flag_ref[0] != 0)
    def _diagonal():
        whole = pltpu.make_async_copy(x_hbm, own_ref, own_sem)
        whole.start()
        whole.wait()
        for b in range(blocks):
            own = own_ref[b, :width, :].astype(jnp.float32) + own_ref[b, width:, :].astype(jnp.float32)
            out_ref[b, :width, :] = own

    @pl.when(flag_ref[0] == 0)
    def _elsewhere():
        out_ref[:, :width, :] = jnp.zeros((blocks, width, edge), jnp.float32)

    def one_slot(s, carry):
        slot = s % 2
        for c in copies(s, slot):
            c.wait()

        @pl.when(s + 1 < count)
        def _next():
            for c in copies(s + 1, 1 - slot):
                c.start()

        i = ids_ref[2 * s]
        both = jnp.dot(xbuf[slot], tbuf[slot], preferred_element_type=jnp.float32)
        out_ref[i, :width, :] += both[:width] + both[width:]
        return carry

    lax.fori_loop(0, count, one_slot, 0)


def _panel_products(ids, cnt, flag, turned, panel, extra):
    slots, edge, _ = turned.shape
    blocks, pair, _ = panel.shape
    width = pair // 2
    height = width + extra.shape[1]
    smem = pl.BlockSpec(memory_space=pltpu.SMEM)
    vmem = pl.BlockSpec(memory_space=pltpu.VMEM)
    hbm = pl.BlockSpec(memory_space=pl.ANY)
    flops = slots * pair * edge * edge * 2
    return pl.pallas_call(
        _tile_kernel,
        in_specs=[smem, smem, smem, hbm, hbm, vmem],
        out_specs=vmem,
        out_shape=jax.ShapeDtypeStruct((blocks, height, edge), jnp.float32),
        scratch_shapes=[
            pltpu.VMEM((blocks, pair, edge), panel.dtype),
            pltpu.VMEM((2, edge, edge), turned.dtype),
            pltpu.VMEM((2, pair, edge), panel.dtype),
            pltpu.SemaphoreType.DMA((2,)),
            pltpu.SemaphoreType.DMA((2,)),
            pltpu.SemaphoreType.DMA,
        ],
        compiler_params=pltpu.CompilerParams(vmem_limit_bytes=56 * 1024 * 1024),
        cost_estimate=pl.CostEstimate(
            flops=flops,
            bytes_accessed=turned.size * 2 + panel.size * 2 + blocks * height * edge * 4,
            transcendentals=0,
        ),
    )(ids, cnt, flag, turned, panel, extra)


def shards(features, weight, tile_values, tile_ids, tile_counts):
    tile_set = tile_values[0, 0]
    slots, edge, _ = tile_set.shape
    slot_ids = tile_ids[0, 0]
    ids = slot_ids.reshape(-1)
    live_count = tile_counts[0, 0]
    cnt = live_count.reshape(1)
    flag = (lax.axis_index("row") == lax.axis_index("col")).astype(jnp.int32).reshape(1)
    turned_w = lax.dot_general(
        weight, features, (((0,), (1,)), ((), ())), precision=lax.Precision.HIGH
    )
    rounded = lax.reduce_precision(turned_w, exponent_bits=8, mantissa_bits=7)
    hi = rounded.astype(jnp.bfloat16)
    lo = (turned_w - rounded).astype(jnp.bfloat16)
    stacked = jnp.concatenate([hi, lo], axis=0)[None]
    panel = lax.all_gather(stacked, "row", axis=0, tiled=True)
    blocks, pair, _ = panel.shape
    width = pair // 2
    turned = jnp.swapaxes(tile_set, 1, 2)
    is_live = (jnp.arange(slots) < live_count).astype(jnp.float32)
    placement = (slot_ids[:, 0][:, None] == jnp.arange(blocks)[None, :]).astype(jnp.float32)
    placement = placement * is_live[:, None]
    tile_sums = jnp.sum(tile_set, axis=2, dtype=jnp.float32)
    row_sums = jnp.dot(placement.T, tile_sums, precision=lax.Precision.HIGHEST)
    extra = jnp.zeros((blocks, EXTRA, edge), jnp.float32).at[:, 0, :].set(row_sums)
    partial = _panel_products(ids, cnt, flag, turned, panel, extra)
    _, height, _ = partial.shape
    mine = lax.psum_scatter(
        partial.reshape(blocks * height, edge), "col", scatter_dimension=0, tiled=True
    )
    degree = 1.0 + mine[width]
    inverse_root = lax.rsqrt(degree)
    return jnp.maximum(mine[:width].T * inverse_root[:, None], 0.0)


def solution(mesh):
    in_specs = (
        P(("col", "row"), None),
        P(),
        P("row", "col", None, None, None),
        P("row", "col", None, None),
        P("row", "col"),
    )
    out_specs = P(("row", "col"), None)
    return jax.shard_map(shards, mesh=mesh, in_specs=in_specs, out_specs=out_specs, check_vma=False)
```

```python
import jax
import jax.numpy as jnp
from jax import lax
from jax.experimental import pallas as pl
from jax.experimental.pallas import tpu as pltpu
from jax.sharding import PartitionSpec as P

EXTRA = 8


def _tile_kernel(ids_ref, cnt_ref, flag_ref, tile_ref, x_ref, extra_ref, out_ref):
    blocks, height, edge = out_ref.shape
    width = x_ref.shape[1] // 2
    out_ref[:, width:, :] = extra_ref[...]

    @pl.when(flag_ref[0] != 0)
    def _diagonal():
        for b in range(blocks):
            own = x_ref[b, :width, :].astype(jnp.float32) + x_ref[b, width:, :].astype(jnp.float32)
            out_ref[b, :width, :] = own

    @pl.when(flag_ref[0] == 0)
    def _elsewhere():
        out_ref[:, :width, :] = jnp.zeros((blocks, width, edge), jnp.float32)

    def one_slot(s, carry):
        i = ids_ref[2 * s]
        j = ids_ref[2 * s + 1]
        both = jnp.dot(x_ref[j], tile_ref[s], preferred_element_type=jnp.float32)
        out_ref[i, :width, :] += both[:width] + both[width:]
        return carry

    lax.fori_loop(0, cnt_ref[0], one_slot, 0)


def _panel_products(ids, cnt, flag, turned, panel, extra):
    slots, edge, _ = turned.shape
    blocks, pair, _ = panel.shape
    width = pair // 2
    height = width + extra.shape[1]
    smem = pl.BlockSpec(memory_space=pltpu.SMEM)
    vmem = pl.BlockSpec(memory_space=pltpu.VMEM)
    flops = slots * pair * edge * edge * 2
    return pl.pallas_call(
        _tile_kernel,
        in_specs=[smem, smem, smem, vmem, vmem, vmem],
        out_specs=vmem,
        out_shape=jax.ShapeDtypeStruct((blocks, height, edge), jnp.float32),
        compiler_params=pltpu.CompilerParams(vmem_limit_bytes=56 * 1024 * 1024),
        cost_estimate=pl.CostEstimate(
            flops=flops,
            bytes_accessed=turned.size * 2 + panel.size * 2 + blocks * height * edge * 4,
            transcendentals=0,
        ),
    )(ids, cnt, flag, turned, panel, extra)


def _split_kernel(x_ref, w_ref, out_ref):
    width = w_ref.shape[1]
    product = jnp.dot(x_ref[...], w_ref[...], precision=lax.Precision.HIGHEST,
                      preferred_element_type=jnp.float32)
    turned = product.T
    hi = turned.astype(jnp.bfloat16)
    out_ref[:width, :] = hi
    out_ref[width:, :] = (turned - hi.astype(jnp.float32)).astype(jnp.bfloat16)


def _split_product(features, weight):
    rows, width = features.shape[0], weight.shape[1]
    vmem = pl.BlockSpec(memory_space=pltpu.VMEM)
    return pl.pallas_call(
        _split_kernel,
        in_specs=[vmem, vmem],
        out_specs=vmem,
        out_shape=jax.ShapeDtypeStruct((2 * width, rows), jnp.bfloat16),
        cost_estimate=pl.CostEstimate(
            flops=rows * weight.shape[0] * width * 2 * 6,
            bytes_accessed=features.size * 4 + weight.size * 4 + 2 * width * rows * 2,
            transcendentals=0,
        ),
    )(features, weight)


def _finish_kernel(mine_ref, out_ref):
    width = out_ref.shape[1]
    scale = lax.rsqrt(1.0 + mine_ref[width:width + 1, :])
    out_ref[...] = jnp.maximum(mine_ref[:width, :] * scale, 0.0).T


def _finish(mine, width):
    edge = mine.shape[1]
    vmem = pl.BlockSpec(memory_space=pltpu.VMEM)
    return pl.pallas_call(
        _finish_kernel,
        in_specs=[vmem],
        out_specs=vmem,
        out_shape=jax.ShapeDtypeStruct((edge, width), jnp.float32),
    )(mine)


def shards(features, weight, tile_values, tile_ids, tile_counts):
    tile_set = tile_values[0, 0]
    slots, edge, _ = tile_set.shape
    slot_ids = tile_ids[0, 0]
    ids = slot_ids.reshape(-1)
    live_count = tile_counts[0, 0]
    cnt = live_count.reshape(1)
    flag = (lax.axis_index("row") == lax.axis_index("col")).astype(jnp.int32).reshape(1)
    stacked = _split_product(features, weight)[None]
    panel = lax.all_gather(stacked, "row", axis=0, tiled=True)
    blocks, pair, _ = panel.shape
    width = pair // 2
    turned = jnp.swapaxes(tile_set, 1, 2)
    is_live = (jnp.arange(slots) < live_count).astype(jnp.float32)
    placement = (slot_ids[:, 0][:, None] == jnp.arange(blocks)[None, :]).astype(jnp.float32)
    placement = placement * is_live[:, None]
    tile_sums = jnp.sum(tile_set, axis=2, dtype=jnp.float32)
    row_sums = jnp.dot(placement.T, tile_sums, precision=lax.Precision.HIGHEST)
    extra = jnp.zeros((blocks, EXTRA, edge), jnp.float32).at[:, 0, :].set(row_sums)
    partial = _panel_products(ids, cnt, flag, turned, panel, extra)
    _, height, _ = partial.shape
    mine = lax.psum_scatter(
        partial.reshape(blocks * height, edge), "col", scatter_dimension=0, tiled=True
    )
    return _finish(mine, width)


def solution(mesh):
    in_specs = (
        P(("col", "row"), None),
        P(),
        P("row", "col", None, None, None),
        P("row", "col", None, None),
        P("row", "col"),
    )
    out_specs = P(("row", "col"), None)
    return jax.shard_map(shards, mesh=mesh, in_specs=in_specs, out_specs=out_specs, check_vma=False)
```

```python
import jax
import jax.numpy as jnp
from jax import lax
from jax.experimental import pallas as pl
from jax.experimental.pallas import tpu as pltpu
from jax.sharding import PartitionSpec as P

EXTRA = 8


def _tile_kernel(ids_ref, cnt_ref, flag_ref, tile_ref, x_ref, extra_ref, out_ref):
    blocks, height, edge = out_ref.shape
    width = x_ref.shape[1]
    out_ref[:, width:, :] = extra_ref[...]

    @pl.when(flag_ref[0] != 0)
    def _diagonal():
        for b in range(blocks):
            own = x_ref[b, :, :edge].astype(jnp.float32) + x_ref[b, :, edge:].astype(jnp.float32)
            out_ref[b, :width, :] = own

    @pl.when(flag_ref[0] == 0)
    def _elsewhere():
        out_ref[:, :width, :] = jnp.zeros((blocks, width, edge), jnp.float32)

    def one_slot(s, carry):
        i = ids_ref[2 * s]
        j = ids_ref[2 * s + 1]
        tile = tile_ref[s]
        stacked = jnp.concatenate([tile, tile], axis=0)
        out_ref[i, :width, :] += jnp.dot(x_ref[j], stacked, preferred_element_type=jnp.float32)
        return carry

    lax.fori_loop(0, cnt_ref[0], one_slot, 0)


def _panel_products(ids, cnt, flag, turned, panel, extra):
    slots, edge, _ = turned.shape
    blocks, width, pair = panel.shape
    height = width + extra.shape[1]
    smem = pl.BlockSpec(memory_space=pltpu.SMEM)
    vmem = pl.BlockSpec(memory_space=pltpu.VMEM)
    flops = slots * pair * edge * edge * 2
    return pl.pallas_call(
        _tile_kernel,
        in_specs=[smem, smem, smem, vmem, vmem, vmem],
        out_specs=vmem,
        out_shape=jax.ShapeDtypeStruct((blocks, height, edge), jnp.float32),
        compiler_params=pltpu.CompilerParams(vmem_limit_bytes=56 * 1024 * 1024),
        cost_estimate=pl.CostEstimate(
            flops=flops,
            bytes_accessed=turned.size * 2 + panel.size * 2 + blocks * height * edge * 4,
            transcendentals=0,
        ),
    )(ids, cnt, flag, turned, panel, extra)


def _split_kernel(x_ref, w_ref, out_ref):
    width = w_ref.shape[1]
    product = jnp.dot(x_ref[...], w_ref[...], precision=lax.Precision.HIGHEST,
                      preferred_element_type=jnp.float32)
    turned = product.T
    rows = turned.shape[1]
    hi = turned.astype(jnp.bfloat16)
    out_ref[:, :rows] = hi
    out_ref[:, rows:] = (turned - hi.astype(jnp.float32)).astype(jnp.bfloat16)


def _split_product(features, weight):
    rows, width = features.shape[0], weight.shape[1]
    vmem = pl.BlockSpec(memory_space=pltpu.VMEM)
    return pl.pallas_call(
        _split_kernel,
        in_specs=[vmem, vmem],
        out_specs=vmem,
        out_shape=jax.ShapeDtypeStruct((width, 2 * rows), jnp.bfloat16),
        cost_estimate=pl.CostEstimate(
            flops=rows * weight.shape[0] * width * 2 * 6,
            bytes_accessed=features.size * 4 + weight.size * 4 + 2 * width * rows * 2,
            transcendentals=0,
        ),
    )(features, weight)


def _finish_kernel(mine_ref, out_ref):
    width = out_ref.shape[1]
    scale = lax.rsqrt(1.0 + mine_ref[width:width + 1, :])
    out_ref[...] = jnp.maximum(mine_ref[:width, :] * scale, 0.0).T


def _finish(mine, width):
    edge = mine.shape[1]
    vmem = pl.BlockSpec(memory_space=pltpu.VMEM)
    return pl.pallas_call(
        _finish_kernel,
        in_specs=[vmem],
        out_specs=vmem,
        out_shape=jax.ShapeDtypeStruct((edge, width), jnp.float32),
    )(mine)


def shards(features, weight, tile_values, tile_ids, tile_counts):
    tile_set = tile_values[0, 0]
    slots, edge, _ = tile_set.shape
    slot_ids = tile_ids[0, 0]
    ids = slot_ids.reshape(-1)
    live_count = tile_counts[0, 0]
    cnt = live_count.reshape(1)
    flag = (lax.axis_index("row") == lax.axis_index("col")).astype(jnp.int32).reshape(1)
    stacked = _split_product(features, weight)[None]
    panel = lax.all_gather(stacked, "row", axis=0, tiled=True)
    blocks, width, _ = panel.shape
    turned = jnp.swapaxes(tile_set, 1, 2)
    is_live = (jnp.arange(slots) < live_count).astype(jnp.float32)
    placement = (slot_ids[:, 0][:, None] == jnp.arange(blocks)[None, :]).astype(jnp.float32)
    placement = placement * is_live[:, None]
    tile_sums = jnp.sum(tile_set, axis=2, dtype=jnp.float32)
    row_sums = jnp.dot(placement.T, tile_sums, precision=lax.Precision.HIGHEST)
    extra = jnp.zeros((blocks, EXTRA, edge), jnp.float32).at[:, 0, :].set(row_sums)
    partial = _panel_products(ids, cnt, flag, turned, panel, extra)
    _, height, _ = partial.shape
    mine = lax.psum_scatter(
        partial.reshape(blocks * height, edge), "col", scatter_dimension=0, tiled=True
    )
    return _finish(mine, width)


def solution(mesh):
    in_specs = (
        P(("col", "row"), None),
        P(),
        P("row", "col", None, None, None),
        P("row", "col", None, None),
        P("row", "col"),
    )
    out_specs = P(("row", "col"), None)
    return jax.shard_map(shards, mesh=mesh, in_specs=in_specs, out_specs=out_specs, check_vma=False)
```

```python
import jax
import jax.numpy as jnp
from jax import lax
from jax.experimental import pallas as pl
from jax.experimental.pallas import tpu as pltpu
from jax.sharding import PartitionSpec as P

EXTRA = 8


def _tile_kernel(ids_ref, cnt_ref, flag_ref, tile_hbm, x_hbm, extra_ref, out_ref,
                 tile_ref, x_ref, tile_sem, x_sem):
    blocks, height, edge = out_ref.shape
    width = x_ref.shape[1] // 2
    count = cnt_ref[0]

    panel_copy = pltpu.make_async_copy(x_hbm, x_ref, x_sem)
    panel_copy.start()

    def tile_copy(s):
        return pltpu.make_async_copy(tile_hbm.at[s], tile_ref.at[s], tile_sem.at[s])

    def start_tile(s, carry):
        tile_copy(s).start()
        return carry

    lax.fori_loop(0, count, start_tile, 0)
    out_ref[:, width:, :] = extra_ref[...]

    @pl.when(flag_ref[0] == 0)
    def _elsewhere():
        out_ref[:, :width, :] = jnp.zeros((blocks, width, edge), jnp.float32)

    panel_copy.wait()

    @pl.when(flag_ref[0] != 0)
    def _diagonal():
        for b in range(blocks):
            own = x_ref[b, :width, :].astype(jnp.float32) + x_ref[b, width:, :].astype(jnp.float32)
            out_ref[b, :width, :] = own

    def one_slot(s, carry):
        tile_copy(s).wait()
        i = ids_ref[2 * s]
        j = ids_ref[2 * s + 1]
        both = jnp.dot(x_ref[j], tile_ref[s], preferred_element_type=jnp.float32)
        out_ref[i, :width, :] += both[:width] + both[width:]
        return carry

    lax.fori_loop(0, count, one_slot, 0)


def _panel_products(ids, cnt, flag, turned, panel, extra):
    slots, edge, _ = turned.shape
    blocks, pair, _ = panel.shape
    width = pair // 2
    height = width + extra.shape[1]
    smem = pl.BlockSpec(memory_space=pltpu.SMEM)
    vmem = pl.BlockSpec(memory_space=pltpu.VMEM)
    hbm = pl.BlockSpec(memory_space=pl.ANY)
    flops = slots * pair * edge * edge * 2
    return pl.pallas_call(
        _tile_kernel,
        in_specs=[smem, smem, smem, hbm, hbm, vmem],
        out_specs=vmem,
        out_shape=jax.ShapeDtypeStruct((blocks, height, edge), jnp.float32),
        scratch_shapes=[
            pltpu.VMEM(turned.shape, turned.dtype),
            pltpu.VMEM(panel.shape, panel.dtype),
            pltpu.SemaphoreType.DMA((slots,)),
            pltpu.SemaphoreType.DMA,
        ],
        compiler_params=pltpu.CompilerParams(vmem_limit_bytes=56 * 1024 * 1024),
        cost_estimate=pl.CostEstimate(
            flops=flops,
            bytes_accessed=turned.size * 2 + panel.size * 2 + blocks * height * edge * 4,
            transcendentals=0,
        ),
    )(ids, cnt, flag, turned, panel, extra)


def _split_kernel(x_ref, w_ref, out_ref):
    width = w_ref.shape[1]
    product = jnp.dot(x_ref[...], w_ref[...], precision=lax.Precision.HIGHEST,
                      preferred_element_type=jnp.float32)
    turned = product.T
    hi = turned.astype(jnp.bfloat16)
    out_ref[:width, :] = hi
    out_ref[width:, :] = (turned - hi.astype(jnp.float32)).astype(jnp.bfloat16)


def _split_product(features, weight):
    rows, width = features.shape[0], weight.shape[1]
    vmem = pl.BlockSpec(memory_space=pltpu.VMEM)
    return pl.pallas_call(
        _split_kernel,
        in_specs=[vmem, vmem],
        out_specs=vmem,
        out_shape=jax.ShapeDtypeStruct((2 * width, rows), jnp.bfloat16),
        cost_estimate=pl.CostEstimate(
            flops=rows * weight.shape[0] * width * 2 * 6,
            bytes_accessed=features.size * 4 + weight.size * 4 + 2 * width * rows * 2,
            transcendentals=0,
        ),
    )(features, weight)


def _finish_kernel(mine_ref, out_ref):
    width = out_ref.shape[1]
    scale = lax.rsqrt(1.0 + mine_ref[width:width + 1, :])
    out_ref[...] = jnp.maximum(mine_ref[:width, :] * scale, 0.0).T


def _finish(mine, width):
    edge = mine.shape[1]
    vmem = pl.BlockSpec(memory_space=pltpu.VMEM)
    return pl.pallas_call(
        _finish_kernel,
        in_specs=[vmem],
        out_specs=vmem,
        out_shape=jax.ShapeDtypeStruct((edge, width), jnp.float32),
    )(mine)


def shards(features, weight, tile_values, tile_ids, tile_counts):
    tile_set = tile_values[0, 0]
    slots, edge, _ = tile_set.shape
    slot_ids = tile_ids[0, 0]
    ids = slot_ids.reshape(-1)
    live_count = tile_counts[0, 0]
    cnt = live_count.reshape(1)
    flag = (lax.axis_index("row") == lax.axis_index("col")).astype(jnp.int32).reshape(1)
    stacked = _split_product(features, weight)[None]
    panel = lax.all_gather(stacked, "row", axis=0, tiled=True)
    blocks, pair, _ = panel.shape
    width = pair // 2
    turned = jnp.swapaxes(tile_set, 1, 2)
    is_live = (jnp.arange(slots) < live_count).astype(jnp.float32)
    placement = (slot_ids[:, 0][:, None] == jnp.arange(blocks)[None, :]).astype(jnp.float32)
    placement = placement * is_live[:, None]
    tile_sums = jnp.sum(tile_set, axis=2, dtype=jnp.float32)
    row_sums = jnp.dot(placement.T, tile_sums, precision=lax.Precision.HIGHEST)
    extra = jnp.zeros((blocks, EXTRA, edge), jnp.float32).at[:, 0, :].set(row_sums)
    partial = _panel_products(ids, cnt, flag, turned, panel, extra)
    _, height, _ = partial.shape
    mine = lax.psum_scatter(
        partial.reshape(blocks * height, edge), "col", scatter_dimension=0, tiled=True
    )
    return _finish(mine, width)


def solution(mesh):
    in_specs = (
        P(("col", "row"), None),
        P(),
        P("row", "col", None, None, None),
        P("row", "col", None, None),
        P("row", "col"),
    )
    out_specs = P(("row", "col"), None)
    return jax.shard_map(shards, mesh=mesh, in_specs=in_specs, out_specs=out_specs, check_vma=False)
```

```python
import jax
import jax.numpy as jnp
from jax import lax
from jax.experimental import pallas as pl
from jax.experimental.pallas import tpu as pltpu
from jax.sharding import PartitionSpec as P

EXTRA = 8


def _tile_kernel(ids_ref, cnt_ref, flag_ref, tile_hbm, x_hbm, extra_ref, out_ref,
                 tile_ref, x_ref, tile_sem, x_sem):
    blocks, height, edge = out_ref.shape
    width = x_ref.shape[1] // 2
    count = cnt_ref[0]

    panel_copy = pltpu.make_async_copy(x_hbm, x_ref, x_sem)
    panel_copy.start()

    def tile_copy(s):
        return pltpu.make_async_copy(tile_hbm.at[s], tile_ref.at[s], tile_sem.at[s])

    def start_tile(s, carry):
        tile_copy(s).start()
        return carry

    lax.fori_loop(0, count, start_tile, 0)
    out_ref[:, width:, :] = extra_ref[...]

    @pl.when(flag_ref[0] == 0)
    def _elsewhere():
        out_ref[:, :width, :] = jnp.zeros((blocks, width, edge), jnp.float32)

    panel_copy.wait()

    @pl.when(flag_ref[0] != 0)
    def _diagonal():
        for b in range(blocks):
            own = x_ref[b, :width, :].astype(jnp.float32) + x_ref[b, width:, :].astype(jnp.float32)
            out_ref[b, :width, :] = own

    def one_slot(s, carry):
        tile_copy(s).wait()
        i = ids_ref[2 * s]
        j = ids_ref[2 * s + 1]
        both = jnp.dot(x_ref[j], tile_ref[s], preferred_element_type=jnp.float32)
        out_ref[i, :width, :] += both[:width] + both[width:]
        return carry

    lax.fori_loop(0, count, one_slot, 0)


def _panel_products(ids, cnt, flag, turned, panel, extra):
    slots, edge, _ = turned.shape
    blocks, pair, _ = panel.shape
    width = pair // 2
    height = width + extra.shape[1]
    smem = pl.BlockSpec(memory_space=pltpu.SMEM)
    vmem = pl.BlockSpec(memory_space=pltpu.VMEM)
    hbm = pl.BlockSpec(memory_space=pl.ANY)
    flops = slots * pair * edge * edge * 2
    return pl.pallas_call(
        _tile_kernel,
        in_specs=[smem, smem, smem, hbm, hbm, vmem],
        out_specs=vmem,
        out_shape=jax.ShapeDtypeStruct((blocks, height, edge), jnp.float32),
        scratch_shapes=[
            pltpu.VMEM(turned.shape, turned.dtype),
            pltpu.VMEM(panel.shape, panel.dtype),
            pltpu.SemaphoreType.DMA((slots,)),
            pltpu.SemaphoreType.DMA,
        ],
        compiler_params=pltpu.CompilerParams(vmem_limit_bytes=56 * 1024 * 1024),
        cost_estimate=pl.CostEstimate(
            flops=flops,
            bytes_accessed=turned.size * 2 + panel.size * 2 + blocks * height * edge * 4,
            transcendentals=0,
        ),
    )(ids, cnt, flag, turned, panel, extra)


def _split_kernel(x_ref, w_ref, out_ref):
    width = w_ref.shape[1]
    x = x_ref[...]
    w = w_ref[...]
    x_hi = x.astype(jnp.bfloat16)
    x_lo = (x - x_hi.astype(jnp.float32)).astype(jnp.bfloat16)
    w_hi = w.astype(jnp.bfloat16)
    w_lo = (w - w_hi.astype(jnp.float32)).astype(jnp.bfloat16)
    product = jnp.dot(x_hi, w_hi, preferred_element_type=jnp.float32)
    product += jnp.dot(x_hi, w_lo, preferred_element_type=jnp.float32)
    product += jnp.dot(x_lo, w_hi, preferred_element_type=jnp.float32)
    turned = product.T
    hi = turned.astype(jnp.bfloat16)
    out_ref[:width, :] = hi
    out_ref[width:, :] = (turned - hi.astype(jnp.float32)).astype(jnp.bfloat16)


def _split_product(features, weight):
    rows, width = features.shape[0], weight.shape[1]
    vmem = pl.BlockSpec(memory_space=pltpu.VMEM)
    return pl.pallas_call(
        _split_kernel,
        in_specs=[vmem, vmem],
        out_specs=vmem,
        out_shape=jax.ShapeDtypeStruct((2 * width, rows), jnp.bfloat16),
        cost_estimate=pl.CostEstimate(
            flops=rows * weight.shape[0] * width * 2 * 3,
            bytes_accessed=features.size * 4 + weight.size * 4 + 2 * width * rows * 2,
            transcendentals=0,
        ),
    )(features, weight)


def _finish_kernel(mine_ref, out_ref):
    width = out_ref.shape[1]
    scale = lax.rsqrt(1.0 + mine_ref[width:width + 1, :])
    out_ref[...] = jnp.maximum(mine_ref[:width, :] * scale, 0.0).T


def _finish(mine, width):
    edge = mine.shape[1]
    vmem = pl.BlockSpec(memory_space=pltpu.VMEM)
    return pl.pallas_call(
        _finish_kernel,
        in_specs=[vmem],
        out_specs=vmem,
        out_shape=jax.ShapeDtypeStruct((edge, width), jnp.float32),
    )(mine)


def shards(features, weight, tile_values, tile_ids, tile_counts):
    tile_set = tile_values[0, 0]
    slots, edge, _ = tile_set.shape
    slot_ids = tile_ids[0, 0]
    ids = slot_ids.reshape(-1)
    live_count = tile_counts[0, 0]
    cnt = live_count.reshape(1)
    flag = (lax.axis_index("row") == lax.axis_index("col")).astype(jnp.int32).reshape(1)
    stacked = _split_product(features, weight)[None]
    panel = lax.all_gather(stacked, "row", axis=0, tiled=True)
    blocks, pair, _ = panel.shape
    width = pair // 2
    turned = jnp.swapaxes(tile_set, 1, 2)
    is_live = (jnp.arange(slots) < live_count).astype(jnp.float32)
    placement = (slot_ids[:, 0][:, None] == jnp.arange(blocks)[None, :]).astype(jnp.float32)
    placement = placement * is_live[:, None]
    tile_sums = jnp.sum(tile_set, axis=2, dtype=jnp.float32)
    row_sums = jnp.dot(placement.T, tile_sums, precision=lax.Precision.HIGHEST)
    extra = jnp.zeros((blocks, EXTRA, edge), jnp.float32).at[:, 0, :].set(row_sums)
    partial = _panel_products(ids, cnt, flag, turned, panel, extra)
    _, height, _ = partial.shape
    mine = lax.psum_scatter(
        partial.reshape(blocks * height, edge), "col", scatter_dimension=0, tiled=True
    )
    return _finish(mine, width)


def solution(mesh):
    in_specs = (
        P(("col", "row"), None),
        P(),
        P("row", "col", None, None, None),
        P("row", "col", None, None),
        P("row", "col"),
    )
    out_specs = P(("row", "col"), None)
    return jax.shard_map(shards, mesh=mesh, in_specs=in_specs, out_specs=out_specs, check_vma=False)
```

```python
import jax
import jax.numpy as jnp
from jax import lax
from jax.experimental import pallas as pl
from jax.experimental.pallas import tpu as pltpu
from jax.sharding import PartitionSpec as P

EXTRA = 8


def _tile_kernel(ids_ref, cnt_ref, flag_ref, tile_hbm, x_hbm, extra_ref, out_ref,
                 tile_ref, x_ref, tile_sem, x_sem):
    blocks, height, edge = out_ref.shape
    width = x_ref.shape[1] // 2
    count = cnt_ref[0]
    half = blocks // 2

    panel_copies = [
        pltpu.make_async_copy(x_hbm.at[pl.ds(h * half, half)], x_ref.at[pl.ds(h * half, half)], x_sem.at[h])
        for h in range(2)
    ]
    for c in panel_copies:
        c.start()

    def tile_copy(s):
        return pltpu.make_async_copy(tile_hbm.at[s], tile_ref.at[s], tile_sem.at[s])

    def start_tile(s, carry):
        tile_copy(s).start()
        return carry

    lax.fori_loop(0, count, start_tile, 0)
    out_ref[:, width:, :] = extra_ref[...]
    out_ref[:, :width, :] = jnp.zeros((blocks, width, edge), jnp.float32)

    def slots_in(h):
        def one_slot(s, carry):
            j = ids_ref[2 * s + 1]

            @pl.when((j >= h * half) & (j < (h + 1) * half))
            def _add():
                tile_copy(s).wait()
                i = ids_ref[2 * s]
                both = jnp.dot(x_ref[j], tile_ref[s], preferred_element_type=jnp.float32)
                out_ref[i, :width, :] += both[:width] + both[width:]

            return carry

        lax.fori_loop(0, count, one_slot, 0)

    for h in range(2):
        panel_copies[h].wait()
        slots_in(h)

    @pl.when(flag_ref[0] != 0)
    def _diagonal():
        for b in range(blocks):
            own = x_ref[b, :width, :].astype(jnp.float32) + x_ref[b, width:, :].astype(jnp.float32)
            out_ref[b, :width, :] += own


def _panel_products(ids, cnt, flag, turned, panel, extra):
    slots, edge, _ = turned.shape
    blocks, pair, _ = panel.shape
    width = pair // 2
    height = width + extra.shape[1]
    smem = pl.BlockSpec(memory_space=pltpu.SMEM)
    vmem = pl.BlockSpec(memory_space=pltpu.VMEM)
    hbm = pl.BlockSpec(memory_space=pl.ANY)
    flops = slots * pair * edge * edge * 2
    return pl.pallas_call(
        _tile_kernel,
        in_specs=[smem, smem, smem, hbm, hbm, vmem],
        out_specs=vmem,
        out_shape=jax.ShapeDtypeStruct((blocks, height, edge), jnp.float32),
        scratch_shapes=[
            pltpu.VMEM(turned.shape, turned.dtype),
            pltpu.VMEM(panel.shape, panel.dtype),
            pltpu.SemaphoreType.DMA((slots,)),
            pltpu.SemaphoreType.DMA((2,)),
        ],
        compiler_params=pltpu.CompilerParams(vmem_limit_bytes=56 * 1024 * 1024),
        cost_estimate=pl.CostEstimate(
            flops=flops,
            bytes_accessed=turned.size * 2 + panel.size * 2 + blocks * height * edge * 4,
            transcendentals=0,
        ),
    )(ids, cnt, flag, turned, panel, extra)


def _split_kernel(x_ref, w_ref, out_ref):
    width = w_ref.shape[1]
    x = x_ref[...]
    w = w_ref[...]
    x_hi = x.astype(jnp.bfloat16)
    x_lo = (x - x_hi.astype(jnp.float32)).astype(jnp.bfloat16)
    w_hi = w.astype(jnp.bfloat16)
    w_lo = (w - w_hi.astype(jnp.float32)).astype(jnp.bfloat16)
    product = jnp.dot(x_hi, w_hi, preferred_element_type=jnp.float32)
    product += jnp.dot(x_hi, w_lo, preferred_element_type=jnp.float32)
    product += jnp.dot(x_lo, w_hi, preferred_element_type=jnp.float32)
    turned = product.T
    hi = turned.astype(jnp.bfloat16)
    out_ref[:width, :] = hi
    out_ref[width:, :] = (turned - hi.astype(jnp.float32)).astype(jnp.bfloat16)


def _split_product(features, weight):
    rows, width = features.shape[0], weight.shape[1]
    vmem = pl.BlockSpec(memory_space=pltpu.VMEM)
    return pl.pallas_call(
        _split_kernel,
        in_specs=[vmem, vmem],
        out_specs=vmem,
        out_shape=jax.ShapeDtypeStruct((2 * width, rows), jnp.bfloat16),
        cost_estimate=pl.CostEstimate(
            flops=rows * weight.shape[0] * width * 2 * 3,
            bytes_accessed=features.size * 4 + weight.size * 4 + 2 * width * rows * 2,
            transcendentals=0,
        ),
    )(features, weight)


def _finish_kernel(mine_ref, out_ref):
    width = out_ref.shape[1]
    scale = lax.rsqrt(1.0 + mine_ref[width:width + 1, :])
    out_ref[...] = jnp.maximum(mine_ref[:width, :] * scale, 0.0).T


def _finish(mine, width):
    edge = mine.shape[1]
    vmem = pl.BlockSpec(memory_space=pltpu.VMEM)
    return pl.pallas_call(
        _finish_kernel,
        in_specs=[vmem],
        out_specs=vmem,
        out_shape=jax.ShapeDtypeStruct((edge, width), jnp.float32),
    )(mine)


def shards(features, weight, tile_values, tile_ids, tile_counts):
    tile_set = tile_values[0, 0]
    slots, edge, _ = tile_set.shape
    slot_ids = tile_ids[0, 0]
    ids = slot_ids.reshape(-1)
    live_count = tile_counts[0, 0]
    cnt = live_count.reshape(1)
    flag = (lax.axis_index("row") == lax.axis_index("col")).astype(jnp.int32).reshape(1)
    stacked = _split_product(features, weight)[None]
    panel = lax.all_gather(stacked, "row", axis=0, tiled=True)
    blocks, pair, _ = panel.shape
    width = pair // 2
    turned = jnp.swapaxes(tile_set, 1, 2)
    is_live = (jnp.arange(slots) < live_count).astype(jnp.float32)
    placement = (slot_ids[:, 0][:, None] == jnp.arange(blocks)[None, :]).astype(jnp.float32)
    placement = placement * is_live[:, None]
    tile_sums = jnp.sum(tile_set, axis=2, dtype=jnp.float32)
    row_sums = jnp.dot(placement.T, tile_sums, precision=lax.Precision.HIGHEST)
    extra = jnp.zeros((blocks, EXTRA, edge), jnp.float32).at[:, 0, :].set(row_sums)
    partial = _panel_products(ids, cnt, flag, turned, panel, extra)
    _, height, _ = partial.shape
    mine = lax.psum_scatter(
        partial.reshape(blocks * height, edge), "col", scatter_dimension=0, tiled=True
    )
    return _finish(mine, width)


def solution(mesh):
    in_specs = (
        P(("col", "row"), None),
        P(),
        P("row", "col", None, None, None),
        P("row", "col", None, None),
        P("row", "col"),
    )
    out_specs = P(("row", "col"), None)
    return jax.shard_map(shards, mesh=mesh, in_specs=in_specs, out_specs=out_specs, check_vma=False)
```

```python
import jax
import jax.numpy as jnp
from jax import lax
from jax.experimental import pallas as pl
from jax.experimental.pallas import tpu as pltpu
from jax.sharding import PartitionSpec as P

EXTRA = 8


def _tile_kernel(ids_ref, cnt_ref, flag_ref, tile_hbm, x_hbm, extra_ref, out_ref,
                 tile_ref, x_ref, tile_sem, x_sem):
    blocks, height, edge = out_ref.shape
    width = x_ref.shape[1] // 2
    count = cnt_ref[0]

    panel_copy = pltpu.make_async_copy(x_hbm, x_ref, x_sem)
    panel_copy.start()

    def tile_copy(s):
        return pltpu.make_async_copy(tile_hbm.at[s], tile_ref.at[s], tile_sem.at[s])

    def start_tile(s, carry):
        tile_copy(s).start()
        return carry

    lax.fori_loop(0, count, start_tile, 0)
    out_ref[:, width:, :] = extra_ref[...]

    @pl.when(flag_ref[0] == 0)
    def _elsewhere():
        out_ref[:, :width, :] = jnp.zeros((blocks, width, edge), jnp.float32)

    panel_copy.wait()

    @pl.when(flag_ref[0] != 0)
    def _diagonal():
        for b in range(blocks):
            own = x_ref[b, :width, :].astype(jnp.float32) + x_ref[b, width:, :].astype(jnp.float32)
            out_ref[b, :width, :] = own

    def one_slot(s, carry):
        tile_copy(s).wait()
        i = ids_ref[2 * s]
        j = ids_ref[2 * s + 1]
        both = jnp.dot(x_ref[j], tile_ref[s], preferred_element_type=jnp.float32)
        out_ref[i, :width, :] += both[:width] + both[width:]
        return carry

    lax.fori_loop(0, count, one_slot, 0)


def _panel_products(ids, cnt, flag, turned, panel, extra):
    slots, edge, _ = turned.shape
    blocks, pair, _ = panel.shape
    width = pair // 2
    height = width + extra.shape[1]
    smem = pl.BlockSpec(memory_space=pltpu.SMEM)
    vmem = pl.BlockSpec(memory_space=pltpu.VMEM)
    hbm = pl.BlockSpec(memory_space=pl.ANY)
    flops = slots * pair * edge * edge * 2
    return pl.pallas_call(
        _tile_kernel,
        in_specs=[smem, smem, smem, hbm, hbm, vmem],
        out_specs=vmem,
        out_shape=jax.ShapeDtypeStruct((blocks, height, edge), jnp.float32),
        scratch_shapes=[
            pltpu.VMEM(turned.shape, turned.dtype),
            pltpu.VMEM(panel.shape, panel.dtype),
            pltpu.SemaphoreType.DMA((slots,)),
            pltpu.SemaphoreType.DMA,
        ],
        compiler_params=pltpu.CompilerParams(vmem_limit_bytes=56 * 1024 * 1024),
        cost_estimate=pl.CostEstimate(
            flops=flops,
            bytes_accessed=turned.size * 2 + panel.size * 2 + blocks * height * edge * 4,
            transcendentals=0,
        ),
    )(ids, cnt, flag, turned, panel, extra)


def _halves(v):
    hi = v.astype(jnp.bfloat16)
    return hi, (v - hi.astype(jnp.float32)).astype(jnp.bfloat16)


def _split_kernel(x_ref, out_ref):
    turned = x_ref[...].T
    width = turned.shape[0]
    hi, lo = _halves(turned)
    out_ref[:width, :] = hi
    out_ref[width:, :] = lo


def _split_rows(features):
    rows, width = features.shape
    vmem = pl.BlockSpec(memory_space=pltpu.VMEM)
    return pl.pallas_call(
        _split_kernel,
        in_specs=[vmem],
        out_specs=vmem,
        out_shape=jax.ShapeDtypeStruct((2 * width, rows), jnp.bfloat16),
    )(features)


def _finish_kernel(mine_ref, w_ref, out_ref):
    width = w_ref.shape[0]
    scale = lax.rsqrt(1.0 + mine_ref[width:width + 1, :])
    scaled = (mine_ref[:width, :] * scale).T
    a_hi, a_lo = _halves(scaled)
    w_hi, w_lo = _halves(w_ref[...])
    product = jnp.dot(a_hi, w_hi, preferred_element_type=jnp.float32)
    product += jnp.dot(a_hi, w_lo, preferred_element_type=jnp.float32)
    product += jnp.dot(a_lo, w_hi, preferred_element_type=jnp.float32)
    out_ref[...] = jnp.maximum(product, 0.0)


def _finish(mine, weight):
    edge = mine.shape[1]
    vmem = pl.BlockSpec(memory_space=pltpu.VMEM)
    return pl.pallas_call(
        _finish_kernel,
        in_specs=[vmem, vmem],
        out_specs=vmem,
        out_shape=jax.ShapeDtypeStruct((edge, weight.shape[1]), jnp.float32),
        cost_estimate=pl.CostEstimate(
            flops=edge * weight.shape[0] * weight.shape[1] * 2 * 3,
            bytes_accessed=mine.size * 4 + weight.size * 4 + edge * weight.shape[1] * 4,
            transcendentals=edge,
        ),
    )(mine, weight)


def shards(features, weight, tile_values, tile_ids, tile_counts):
    tile_set = tile_values[0, 0]
    slots, edge, _ = tile_set.shape
    slot_ids = tile_ids[0, 0]
    ids = slot_ids.reshape(-1)
    live_count = tile_counts[0, 0]
    cnt = live_count.reshape(1)
    flag = (lax.axis_index("row") == lax.axis_index("col")).astype(jnp.int32).reshape(1)
    stacked = _split_rows(features)[None]
    panel = lax.all_gather(stacked, "row", axis=0, tiled=True)
    blocks, pair, _ = panel.shape
    width = pair // 2
    turned = jnp.swapaxes(tile_set, 1, 2)
    is_live = (jnp.arange(slots) < live_count).astype(jnp.float32)
    placement = (slot_ids[:, 0][:, None] == jnp.arange(blocks)[None, :]).astype(jnp.float32)
    placement = placement * is_live[:, None]
    tile_sums = jnp.sum(tile_set, axis=2, dtype=jnp.float32)
    row_sums = jnp.dot(placement.T, tile_sums, precision=lax.Precision.HIGHEST)
    extra = jnp.zeros((blocks, EXTRA, edge), jnp.float32).at[:, 0, :].set(row_sums)
    partial = _panel_products(ids, cnt, flag, turned, panel, extra)
    _, height, _ = partial.shape
    mine = lax.psum_scatter(
        partial.reshape(blocks * height, edge), "col", scatter_dimension=0, tiled=True
    )
    return _finish(mine, weight)


def solution(mesh):
    in_specs = (
        P(("col", "row"), None),
        P(),
        P("row", "col", None, None, None),
        P("row", "col", None, None),
        P("row", "col"),
    )
    out_specs = P(("row", "col"), None)
    return jax.shard_map(shards, mesh=mesh, in_specs=in_specs, out_specs=out_specs, check_vma=False)
```

```python
import jax
import jax.numpy as jnp
from jax import lax
from jax.experimental import pallas as pl
from jax.experimental.pallas import tpu as pltpu
from jax.sharding import PartitionSpec as P

EXTRA = 8


def _tile_kernel(ids_ref, cnt_ref, flag_ref, tile_hbm, x_hbm, extra_ref, out_hbm,
                 tile_ref, x_ref, out_ref, tile_sem, x_sem, out_sem):
    blocks, height, edge = out_ref.shape
    width = x_ref.shape[1] // 2
    count = cnt_ref[0]
    parts = x_sem.shape[0]
    share = blocks // parts

    def chunk(ref, p):
        return ref.at[pl.ds(p * share, share)]

    panel_copies = [
        pltpu.make_async_copy(chunk(x_hbm, p), chunk(x_ref, p), x_sem.at[p]) for p in range(parts)
    ]
    for c in panel_copies:
        c.start()

    def tile_copy(s):
        return pltpu.make_async_copy(tile_hbm.at[s], tile_ref.at[s], tile_sem.at[s])

    def start_tile(s, carry):
        tile_copy(s).start()
        return carry

    lax.fori_loop(0, count, start_tile, 0)
    out_ref[:, width:, :] = extra_ref[...]

    @pl.when(flag_ref[0] == 0)
    def _elsewhere():
        out_ref[:, :width, :] = jnp.zeros((blocks, width, edge), jnp.float32)

    for c in panel_copies:
        c.wait()

    @pl.when(flag_ref[0] != 0)
    def _diagonal():
        for b in range(blocks):
            own = x_ref[b, :width, :].astype(jnp.float32) + x_ref[b, width:, :].astype(jnp.float32)
            out_ref[b, :width, :] = own

    def one_slot(s, carry):
        tile_copy(s).wait()
        i = ids_ref[2 * s]
        j = ids_ref[2 * s + 1]
        both = jnp.dot(x_ref[j], tile_ref[s], preferred_element_type=jnp.float32)
        out_ref[i, :width, :] += both[:width] + both[width:]
        return carry

    lax.fori_loop(0, count, one_slot, 0)
    out_copies = [
        pltpu.make_async_copy(chunk(out_ref, p), chunk(out_hbm, p), out_sem.at[p]) for p in range(parts)
    ]
    for c in out_copies:
        c.start()
    for c in out_copies:
        c.wait()


def _panel_products(ids, cnt, flag, turned, panel, extra):
    slots, edge, _ = turned.shape
    blocks, pair, _ = panel.shape
    width = pair // 2
    height = width + extra.shape[1]
    smem = pl.BlockSpec(memory_space=pltpu.SMEM)
    vmem = pl.BlockSpec(memory_space=pltpu.VMEM)
    hbm = pl.BlockSpec(memory_space=pl.ANY)
    flops = slots * pair * edge * edge * 2
    return pl.pallas_call(
        _tile_kernel,
        in_specs=[smem, smem, smem, hbm, hbm, vmem],
        out_specs=hbm,
        out_shape=jax.ShapeDtypeStruct((blocks, height, edge), jnp.float32),
        scratch_shapes=[
            pltpu.VMEM(turned.shape, turned.dtype),
            pltpu.VMEM(panel.shape, panel.dtype),
            pltpu.VMEM((blocks, height, edge), jnp.float32),
            pltpu.SemaphoreType.DMA((slots,)),
            pltpu.SemaphoreType.DMA((4,)),
            pltpu.SemaphoreType.DMA((4,)),
        ],
        compiler_params=pltpu.CompilerParams(vmem_limit_bytes=56 * 1024 * 1024),
        cost_estimate=pl.CostEstimate(
            flops=flops,
            bytes_accessed=turned.size * 2 + panel.size * 2 + blocks * height * edge * 4,
            transcendentals=0,
        ),
    )(ids, cnt, flag, turned, panel, extra)


def _split_kernel(x_ref, w_ref, out_ref):
    width = w_ref.shape[1]
    x = x_ref[...]
    w = w_ref[...]
    x_hi = x.astype(jnp.bfloat16)
    x_lo = (x - x_hi.astype(jnp.float32)).astype(jnp.bfloat16)
    w_hi = w.astype(jnp.bfloat16)
    w_lo = (w - w_hi.astype(jnp.float32)).astype(jnp.bfloat16)
    product = jnp.dot(x_hi, w_hi, preferred_element_type=jnp.float32)
    product += jnp.dot(x_hi, w_lo, preferred_element_type=jnp.float32)
    product += jnp.dot(x_lo, w_hi, preferred_element_type=jnp.float32)
    turned = product.T
    hi = turned.astype(jnp.bfloat16)
    out_ref[:width, :] = hi
    out_ref[width:, :] = (turned - hi.astype(jnp.float32)).astype(jnp.bfloat16)


def _split_product(features, weight):
    rows, width = features.shape[0], weight.shape[1]
    vmem = pl.BlockSpec(memory_space=pltpu.VMEM)
    return pl.pallas_call(
        _split_kernel,
        in_specs=[vmem, vmem],
        out_specs=vmem,
        out_shape=jax.ShapeDtypeStruct((2 * width, rows), jnp.bfloat16),
        cost_estimate=pl.CostEstimate(
            flops=rows * weight.shape[0] * width * 2 * 3,
            bytes_accessed=features.size * 4 + weight.size * 4 + 2 * width * rows * 2,
            transcendentals=0,
        ),
    )(features, weight)


def _finish_kernel(mine_ref, out_ref):
    width = out_ref.shape[1]
    scale = lax.rsqrt(1.0 + mine_ref[width:width + 1, :])
    out_ref[...] = jnp.maximum(mine_ref[:width, :] * scale, 0.0).T


def _finish(mine, width):
    edge = mine.shape[1]
    vmem = pl.BlockSpec(memory_space=pltpu.VMEM)
    return pl.pallas_call(
        _finish_kernel,
        in_specs=[vmem],
        out_specs=vmem,
        out_shape=jax.ShapeDtypeStruct((edge, width), jnp.float32),
    )(mine)


def shards(features, weight, tile_values, tile_ids, tile_counts):
    tile_set = tile_values[0, 0]
    slots, edge, _ = tile_set.shape
    slot_ids = tile_ids[0, 0]
    ids = slot_ids.reshape(-1)
    live_count = tile_counts[0, 0]
    cnt = live_count.reshape(1)
    flag = (lax.axis_index("row") == lax.axis_index("col")).astype(jnp.int32).reshape(1)
    stacked = _split_product(features, weight)[None]
    panel = lax.all_gather(stacked, "row", axis=0, tiled=True)
    blocks, pair, _ = panel.shape
    width = pair // 2
    turned = jnp.swapaxes(tile_set, 1, 2)
    is_live = (jnp.arange(slots) < live_count).astype(jnp.float32)
    placement = (slot_ids[:, 0][:, None] == jnp.arange(blocks)[None, :]).astype(jnp.float32)
    placement = placement * is_live[:, None]
    tile_sums = jnp.sum(tile_set, axis=2, dtype=jnp.float32)
    row_sums = jnp.dot(placement.T, tile_sums, precision=lax.Precision.HIGHEST)
    extra = jnp.zeros((blocks, EXTRA, edge), jnp.float32).at[:, 0, :].set(row_sums)
    partial = _panel_products(ids, cnt, flag, turned, panel, extra)
    _, height, _ = partial.shape
    mine = lax.psum_scatter(
        partial.reshape(blocks * height, edge), "col", scatter_dimension=0, tiled=True
    )
    return _finish(mine, width)


def solution(mesh):
    in_specs = (
        P(("col", "row"), None),
        P(),
        P("row", "col", None, None, None),
        P("row", "col", None, None),
        P("row", "col"),
    )
    out_specs = P(("row", "col"), None)
    return jax.shard_map(shards, mesh=mesh, in_specs=in_specs, out_specs=out_specs, check_vma=False)
```

```python
import jax
import jax.numpy as jnp
from jax import lax
from jax.experimental import pallas as pl
from jax.experimental.pallas import tpu as pltpu
from jax.sharding import PartitionSpec as P

EXTRA = 8


def _tile_kernel(ids_ref, cnt_ref, flag_ref, tile_hbm, x_hbm, extra_ref, out_hbm,
                 tile_ref, x_ref, out_ref, tile_sem, x_sem, out_sem, waited):
    blocks, height, edge = out_ref.shape
    width = x_ref.shape[1] // 2
    count = cnt_ref[0]
    parts = x_sem.shape[0]
    share = blocks // parts

    def chunk(ref, p):
        return ref.at[pl.ds(p * share, share)]

    panel_copies = [
        pltpu.make_async_copy(chunk(x_hbm, p), chunk(x_ref, p), x_sem.at[p]) for p in range(parts)
    ]
    for c in panel_copies:
        c.start()

    def tile_copy(s):
        return pltpu.make_async_copy(tile_hbm.at[s], tile_ref.at[s], tile_sem.at[s])

    def start_tile(s, carry):
        tile_copy(s).start()
        return carry

    lax.fori_loop(0, count, start_tile, 0)
    out_ref[:, width:, :] = extra_ref[...]

    @pl.when(flag_ref[0] == 0)
    def _elsewhere():
        out_ref[:, :width, :] = jnp.zeros((blocks, width, edge), jnp.float32)

    for p in range(parts):
        waited[p] = 0

    def ensure(p):
        @pl.when(waited[p] == 0)
        def _wait():
            pltpu.make_async_copy(chunk(x_hbm, p), chunk(x_ref, p), x_sem.at[p]).wait()
            waited[p] = 1

    @pl.when(flag_ref[0] != 0)
    def _diagonal():
        for p in range(parts):
            ensure(p)
        for b in range(blocks):
            own = x_ref[b, :width, :].astype(jnp.float32) + x_ref[b, width:, :].astype(jnp.float32)
            out_ref[b, :width, :] = own

    def one_slot(s, carry):
        tile_copy(s).wait()
        i = ids_ref[2 * s]
        j = ids_ref[2 * s + 1]
        ensure(j // share)
        both = jnp.dot(x_ref[j], tile_ref[s], preferred_element_type=jnp.float32)
        out_ref[i, :width, :] += both[:width] + both[width:]
        return carry

    lax.fori_loop(0, count, one_slot, 0)
    for p in range(parts):
        ensure(p)
    out_copies = [
        pltpu.make_async_copy(chunk(out_ref, p), chunk(out_hbm, p), out_sem.at[p]) for p in range(parts)
    ]
    for c in out_copies:
        c.start()
    for c in out_copies:
        c.wait()


def _panel_products(ids, cnt, flag, turned, panel, extra):
    slots, edge, _ = turned.shape
    blocks, pair, _ = panel.shape
    width = pair // 2
    height = width + extra.shape[1]
    smem = pl.BlockSpec(memory_space=pltpu.SMEM)
    vmem = pl.BlockSpec(memory_space=pltpu.VMEM)
    hbm = pl.BlockSpec(memory_space=pl.ANY)
    flops = slots * pair * edge * edge * 2
    return pl.pallas_call(
        _tile_kernel,
        in_specs=[smem, smem, smem, hbm, hbm, vmem],
        out_specs=hbm,
        out_shape=jax.ShapeDtypeStruct((blocks, height, edge), jnp.float32),
        scratch_shapes=[
            pltpu.VMEM(turned.shape, turned.dtype),
            pltpu.VMEM(panel.shape, panel.dtype),
            pltpu.VMEM((blocks, height, edge), jnp.float32),
            pltpu.SemaphoreType.DMA((slots,)),
            pltpu.SemaphoreType.DMA((4,)),
            pltpu.SemaphoreType.DMA((4,)),
            pltpu.SMEM((4,), jnp.int32),
        ],
        compiler_params=pltpu.CompilerParams(vmem_limit_bytes=56 * 1024 * 1024),
        cost_estimate=pl.CostEstimate(
            flops=flops,
            bytes_accessed=turned.size * 2 + panel.size * 2 + blocks * height * edge * 4,
            transcendentals=0,
        ),
    )(ids, cnt, flag, turned, panel, extra)


def _split_kernel(x_ref, w_ref, out_ref):
    width = w_ref.shape[1]
    x = x_ref[...]
    w = w_ref[...]
    x_hi = x.astype(jnp.bfloat16)
    x_lo = (x - x_hi.astype(jnp.float32)).astype(jnp.bfloat16)
    w_hi = w.astype(jnp.bfloat16)
    w_lo = (w - w_hi.astype(jnp.float32)).astype(jnp.bfloat16)
    product = jnp.dot(x_hi, w_hi, preferred_element_type=jnp.float32)
    product += jnp.dot(x_hi, w_lo, preferred_element_type=jnp.float32)
    product += jnp.dot(x_lo, w_hi, preferred_element_type=jnp.float32)
    turned = product.T
    hi = turned.astype(jnp.bfloat16)
    out_ref[:width, :] = hi
    out_ref[width:, :] = (turned - hi.astype(jnp.float32)).astype(jnp.bfloat16)


def _split_product(features, weight):
    rows, width = features.shape[0], weight.shape[1]
    vmem = pl.BlockSpec(memory_space=pltpu.VMEM)
    return pl.pallas_call(
        _split_kernel,
        in_specs=[vmem, vmem],
        out_specs=vmem,
        out_shape=jax.ShapeDtypeStruct((2 * width, rows), jnp.bfloat16),
        cost_estimate=pl.CostEstimate(
            flops=rows * weight.shape[0] * width * 2 * 3,
            bytes_accessed=features.size * 4 + weight.size * 4 + 2 * width * rows * 2,
            transcendentals=0,
        ),
    )(features, weight)


def _finish_kernel(mine_ref, out_ref):
    width = out_ref.shape[1]
    scale = lax.rsqrt(1.0 + mine_ref[width:width + 1, :])
    out_ref[...] = jnp.maximum(mine_ref[:width, :] * scale, 0.0).T


def _finish(mine, width):
    edge = mine.shape[1]
    vmem = pl.BlockSpec(memory_space=pltpu.VMEM)
    return pl.pallas_call(
        _finish_kernel,
        in_specs=[vmem],
        out_specs=vmem,
        out_shape=jax.ShapeDtypeStruct((edge, width), jnp.float32),
    )(mine)


def shards(features, weight, tile_values, tile_ids, tile_counts):
    tile_set = tile_values[0, 0]
    slots, edge, _ = tile_set.shape
    slot_ids = tile_ids[0, 0]
    ids = slot_ids.reshape(-1)
    live_count = tile_counts[0, 0]
    cnt = live_count.reshape(1)
    flag = (lax.axis_index("row") == lax.axis_index("col")).astype(jnp.int32).reshape(1)
    stacked = _split_product(features, weight)[None]
    panel = lax.all_gather(stacked, "row", axis=0, tiled=True)
    blocks, pair, _ = panel.shape
    width = pair // 2
    turned = jnp.swapaxes(tile_set, 1, 2)
    is_live = (jnp.arange(slots) < live_count).astype(jnp.float32)
    placement = (slot_ids[:, 0][:, None] == jnp.arange(blocks)[None, :]).astype(jnp.float32)
    placement = placement * is_live[:, None]
    tile_sums = jnp.sum(tile_set, axis=2, dtype=jnp.float32)
    row_sums = jnp.dot(placement.T, tile_sums, precision=lax.Precision.HIGHEST)
    extra = jnp.zeros((blocks, EXTRA, edge), jnp.float32).at[:, 0, :].set(row_sums)
    partial = _panel_products(ids, cnt, flag, turned, panel, extra)
    _, height, _ = partial.shape
    mine = lax.psum_scatter(
        partial.reshape(blocks * height, edge), "col", scatter_dimension=0, tiled=True
    )
    return _finish(mine, width)


def solution(mesh):
    in_specs = (
        P(("col", "row"), None),
        P(),
        P("row", "col", None, None, None),
        P("row", "col", None, None),
        P("row", "col"),
    )
    out_specs = P(("row", "col"), None)
    return jax.shard_map(shards, mesh=mesh, in_specs=in_specs, out_specs=out_specs, check_vma=False)
```
